512 devices in a mesh: ctx: 64 (over z, x_hi, core), head: 8 (over y, x_lo).
Axes of the slice: x: 4 (x_hi: 2, x_lo: 2; x = x_hi * 2 + x_lo), y: 4, z: 16, core: 2. Of those that a mesh axis runs over, the one named last changes fastest.
Arguments:
- tokens: bfloat16 [8192, 4096], P('ctx'), may hold values from -6 to 6
- norm_gain: float32 [4096], replicated, may hold values from 0.25 to 1.75
- w_query: bfloat16 [4096, 4096], P('ctx', 'head'), may hold values from -0.09375 to 0.09375
- w_key: bfloat16 [4096, 1024], P('ctx', 'head'), may hold values from -0.09375 to 0.09375
- w_value: bfloat16 [4096, 1024], P('ctx', 'head'), may hold values from -0.09375 to 0.09375
- w_out: bfloat16 [4096, 4096], P('head', 'ctx'), may hold values from -0.09375 to 0.09375
- row_map: int32 [8192], P('ctx'), may hold values from 0 to 8191, as said below
- doc_lengths: int32 [32], replicated, may hold values from 1 to 2048, 8192 in all
- doc_labels: int32 [32], replicated, may hold values from 0 to 1, as said below
Outputs:
- residual_out: bfloat16 [8192, 4096], P('ctx', 'head')
- refusal_direction: float32 [4096], P('head')
The draws below stay inside these ranges and needn't reach their ends.
Inputs may be any that keep to these rules, and one draw needn't show every extreme that they name: `row_map`: the rows of ctx index c are two runs of 64 consecutive positions, run b(c) and run 2 * 64 - 1 - b(c) of the pack, b a permutation drawn from the seed; every position appears once. `doc_labels`: at least one prompt of each class.
All inputs are finite; a program needn't handle non-finite values.
Results may differ from the reference program's by a relative error of at most 0.008.
Values may be sent and summed in bfloat16 or wider, within the bound.
No kernel may reach another device: no remote copies, remote signals or barrier semaphores. Data moves between devices by JAX's collectives and lax.ppermute only.
A program may use at most 64 MiB of HBM per device.

```python
import math
import jax
import jax.numpy as jnp
import numpy as np
from jax import lax

D = 4096
HEADS = 32
KV_HEADS = 8
HEAD_DIM = 128
TOK_DEV = 128
TOKENS = 8192
MOST = 2048
NDOCS = 32


def draw_row_map(key, part):
    shard_count = TOKENS // TOK_DEV
    half_len = TOK_DEV // 2
    shard_order = jax.random.permutation(key, shard_count).astype(jnp.int32)
    run_pairs = jnp.stack([shard_order, 2 * shard_count - 1 - shard_order], 1)
    within_run = jnp.arange(half_len, dtype=jnp.int32)
    positions = run_pairs[:, :, None] * half_len + within_run[None, None, :]
    return positions.reshape(TOKENS).astype(jnp.int32)


def draw_doc_labels(key, part):
    count_key, order_key = jax.random.split(key)
    harmful_count = jax.random.randint(count_key, (), 1, NDOCS).astype(jnp.int32)
    prompt_order = jax.random.permutation(order_key, NDOCS).astype(jnp.int32)
    return (prompt_order < harmful_count).astype(jnp.int32)


def steps_of(stream_key, extent, cuts, smallest, top_value):
    gain, own = 1.0, jax.random.fold_in(stream_key, 6)
    for position, parts in cuts:
        draws = jnp.exp(jax.random.uniform(jax.random.fold_in(own, position), (parts,), jnp.float32, smallest / len(cuts), top_value / len(cuts)))
        gain = gain * jnp.repeat(draws, extent[position] // parts).reshape([-1 if axis == position else 1 for axis in range(len(extent))])
    return gain


def profile(amount, total, reach, skew):
    portions = [(1 << 20) // math.isqrt(rank ** skew) + 1 for rank in range(2, amount + 1)]
    surplus, holding = total - reach - (amount - 1), [1] * (amount - 1)
    while surplus > 0:
        movable = [i for i in range(amount - 1) if holding[i] < reach]
        whole, left = sum([portions[i] for i in movable]), surplus
        for i in movable:
            addition = min(reach - holding[i], max(1, left * portions[i] // whole), surplus)
            holding[i] = holding[i] + addition
            surplus = surplus - addition
    return np.array([reach] + holding)


def uneven(key, count, total, bound, lean):
    if count == 2:
        one = jax.random.randint(key, (), max(1, total - bound), min(bound, total - 1) + 1)
        return jnp.stack([one, total - one])
    sizes = jnp.asarray(profile(count, total, bound, lean), jnp.int32)
    pairs = (count - 1) // 2
    giver, receiver = sizes[1:1 + 2 * pairs:2], sizes[2:2 + 2 * pairs:2]
    slack = jnp.minimum(giver - 1, bound - receiver)
    moved = jax.random.randint(jax.random.fold_in(key, 1), (pairs,), 0, 1 << 20) % (slack + 1)
    sizes = sizes.at[1:1 + 2 * pairs:2].set(giver - moved).at[2:2 + 2 * pairs:2].set(receiver + moved)
    return sizes[jax.random.permutation(jax.random.fold_in(key, 2), count)]


def noise(key, shape, deviation, limit, cuts=(), kind=jnp.bfloat16):
    values = jax.random.normal(key, shape, jnp.float32) * deviation
    if len(cuts) > 0:
        values = steps_of(key, shape, cuts, -0.22, 0.18) * values
    return jnp.clip(values, min=-limit, max=limit).astype(kind)


def setup_inputs(seed: int = 0) -> dict:
    seeds = jax.random.split(jax.random.key(seed), 10)
    return {
        "tokens": noise(seeds[0], (TOKENS, D), 1.0, 6.0, ((0, 64),)),
        "norm_gain": jnp.clip(1.0 + 0.15 * jax.random.normal(seeds[1], (D,), jnp.float32), 0.25, 1.75),
        "w_query": noise(seeds[2], (D, HEADS * HEAD_DIM), D ** -0.5, 0.09375, ((0, 64), (1, 8))),
        "w_key": noise(seeds[3], (D, KV_HEADS * HEAD_DIM), D ** -0.5, 0.09375, ((0, 64), (1, 8))),
        "w_value": noise(seeds[4], (D, KV_HEADS * HEAD_DIM), D ** -0.5, 0.09375, ((0, 64), (1, 8))),
        "w_out": noise(seeds[5], (HEADS * HEAD_DIM, D), (HEADS * HEAD_DIM) ** -0.5, 0.09375, ((0, 8), (1, 64))),
        "row_map": draw_row_map(jax.random.fold_in(seeds[9], 71), 0),
        "doc_lengths": uneven(seeds[7], NDOCS, TOKENS, MOST, 2).astype(jnp.int32),
        "doc_labels": draw_doc_labels(jax.random.fold_in(seeds[9], 71), 0),
    }


ROPE_BASE = 500000.0
NEG_FILL = -1e+30

def doc_layout(row_map, doc_lengths):
    doc_ends = jnp.cumsum(doc_lengths).astype(jnp.int32)
    doc_starts = (doc_ends - doc_lengths).astype(jnp.int32)
    doc_index = lax.optimization_barrier(jnp.sum((row_map[:, None] >= doc_ends[None, :]).astype(jnp.int32), 1)).astype(jnp.int32)
    member = doc_index[:, None] == jnp.arange(doc_ends.shape[0], dtype=jnp.int32)[None, :]
    in_doc = (row_map - lax.optimization_barrier(jnp.sum(jnp.where(member, doc_starts[None, :], 0), 1))).astype(jnp.int32)
    return (doc_index, in_doc, doc_ends)

def rotate(values, in_doc):
    head_dim = values.shape[-1]
    half_dim = head_dim // 2
    inv_freq = jnp.exp(jnp.arange(half_dim).astype(jnp.float32) * (-2.0 * math.log(ROPE_BASE) / head_dim))
    angles = in_doc.astype(jnp.float32)[:, None] * inv_freq[None, :]
    shape_out = (angles.shape[0],) + (1,) * (values.ndim - 2) + (half_dim,)
    cosine = jnp.cos(angles).reshape(shape_out)
    sine_val = jnp.sin(angles).reshape(shape_out)
    front_half = values[..., :half_dim]
    back_half = values[..., half_dim:]
    return jnp.concatenate([front_half * cosine - back_half * sine_val, back_half * cosine + front_half * sine_val], -1)

def rms_norm(tokens, norm_gain):
    wide_tokens = tokens.astype(jnp.float32)
    row_scale = lax.rsqrt(lax.optimization_barrier(jnp.mean(wide_tokens * wide_tokens, -1, keepdims=True)) + 1e-05)
    return (wide_tokens * row_scale * norm_gain).astype(jnp.bfloat16)

def reference(tokens, norm_gain, w_query, w_key, w_value, w_out, row_map, doc_lengths, doc_labels):
    normed = rms_norm(tokens, norm_gain)
    doc_index, in_doc, doc_ends = doc_layout(row_map, doc_lengths)
    queries = jnp.dot(normed, w_query, preferred_element_type=jnp.float32).reshape(TOKENS, HEADS, HEAD_DIM)
    key_proj = jnp.dot(normed, w_key, preferred_element_type=jnp.float32).reshape(TOKENS, KV_HEADS, HEAD_DIM)
    value_proj = jnp.dot(normed, w_value, preferred_element_type=jnp.float32).reshape(TOKENS, KV_HEADS, HEAD_DIM).astype(jnp.bfloat16)
    queries = rotate(queries, in_doc).astype(jnp.bfloat16)
    key_proj = rotate(key_proj, in_doc).astype(jnp.bfloat16)
    group_size = HEADS // KV_HEADS
    nat_query = jnp.zeros_like(queries).at[row_map].set(queries)
    nat_key = jnp.zeros_like(key_proj).at[row_map].set(key_proj)
    nat_value = jnp.zeros_like(value_proj).at[row_map].set(value_proj)
    nat_doc = jnp.zeros_like(doc_index).at[row_map].set(doc_index)
    nat_pos = jnp.arange(TOKENS, dtype=jnp.int32)
    window = MOST + TOK_DEV
    nblocks = TOKENS // TOK_DEV
    scale_factor = HEAD_DIM ** (-0.5)

    def one_head(head_number):
        kv_number = head_number // group_size
        q_head = lax.dynamic_index_in_dim(nat_query, head_number, 1, False)
        k_head = lax.dynamic_index_in_dim(nat_key, kv_number, 1, False)
        v_head = lax.dynamic_index_in_dim(nat_value, kv_number, 1, False)

        def one_block(block_number):
            first_row = (block_number * TOK_DEV).astype(jnp.int32)
            win_start = jnp.maximum(first_row + TOK_DEV - window, 0).astype(jnp.int32)
            q_block = lax.dynamic_slice_in_dim(q_head, first_row, TOK_DEV, 0)
            q_pos = lax.dynamic_slice_in_dim(nat_pos, first_row, TOK_DEV, 0)
            q_doc = lax.dynamic_slice_in_dim(nat_doc, first_row, TOK_DEV, 0)
            k_win = lax.dynamic_slice_in_dim(k_head, win_start, window, 0)
            v_win = lax.dynamic_slice_in_dim(v_head, win_start, window, 0)
            k_pos = lax.dynamic_slice_in_dim(nat_pos, win_start, window, 0)
            k_doc = lax.dynamic_slice_in_dim(nat_doc, win_start, window, 0)
            scores = jnp.dot(q_block, k_win.T, preferred_element_type=jnp.float32) * scale_factor
            allowed = (k_doc[None, :] == q_doc[:, None]) & (k_pos[None, :] <= q_pos[:, None])
            scores = jnp.where(allowed, scores, NEG_FILL)
            row_top = lax.optimization_barrier(jnp.max(scores, -1, keepdims=True))
            weights = jnp.where(allowed, jnp.exp(scores - row_top), 0.0)
            row_sum = lax.optimization_barrier(jnp.sum(weights, -1, keepdims=True))
            mixed_rows = jnp.dot(weights.astype(jnp.bfloat16), v_win, preferred_element_type=jnp.float32) / row_sum
            return mixed_rows.astype(jnp.bfloat16)
        result = lax.map(one_block, jnp.arange(nblocks, dtype=jnp.int32))
        return result.reshape(TOKENS, HEAD_DIM)
    attended = lax.map(one_head, jnp.arange(HEADS, dtype=jnp.int32))
    attended = jnp.transpose(attended, (1, 0, 2))[row_map].reshape(TOKENS, HEADS * HEAD_DIM)
    residual_out = (tokens.astype(jnp.float32) + jnp.dot(attended, w_out, preferred_element_type=jnp.float32)).astype(jnp.bfloat16)
    is_last = row_map[:, None] == (doc_ends - 1)[None, :]
    label_f = doc_labels.astype(jnp.float32)
    harmful = jnp.sum(label_f)
    harmless = doc_labels.shape[0] - jnp.sum(label_f)
    row_weight = lax.optimization_barrier(jnp.sum(jnp.where(is_last, (label_f / harmful - (1.0 - label_f) / harmless)[None, :], 0.0), 1))
    refusal_direction = lax.optimization_barrier(jnp.sum(row_weight[:, None] * residual_out.astype(jnp.float32), 0))
    return (residual_out, refusal_direction)
```

```python
import math

import jax
import jax.numpy as jnp
from jax import lax
from jax.sharding import Mesh
from jax.sharding import PartitionSpec as P

HEADS = 32
KV_HEADS = 8
HEAD_DIM = 128
MOST = 2048
RUN = 64

ROPE_BASE = 500000.0
NEG_FILL = -1e30

CTX = ("z", "xh", "c")
HEAD = ("y", "xl")
GATHER_ORDER = ("z", "xh", "c")


def doc_layout(row_map, doc_lengths):
    doc_ends = jnp.cumsum(doc_lengths)
    doc_starts = doc_ends - doc_lengths
    doc_index = jnp.sum((row_map[:, None] >= doc_ends[None, :]).astype(jnp.int32), 1)
    member = doc_index[:, None] == jnp.arange(doc_ends.shape[0], dtype=jnp.int32)[None, :]
    in_doc = row_map - jnp.sum(jnp.where(member, doc_starts[None, :], 0), 1)
    return (doc_index, in_doc, doc_ends)


def rotate(values, in_doc):
    head_dim = values.shape[-1]
    half_dim = head_dim // 2
    inv_freq = jnp.exp(
        jnp.arange(half_dim).astype(jnp.float32) * (-2.0 * math.log(ROPE_BASE) / head_dim)
    )
    angles = in_doc.astype(jnp.float32)[:, None] * inv_freq[None, :]
    shape_out = (angles.shape[0],) + (1,) * (values.ndim - 2) + (half_dim,)
    cosine = jnp.cos(angles).reshape(shape_out)
    sine_val = jnp.sin(angles).reshape(shape_out)
    front_half = values[..., :half_dim]
    back_half = values[..., half_dim:]
    return jnp.concatenate(
        [front_half * cosine - back_half * sine_val, back_half * cosine + front_half * sine_val], -1
    )


def rms_norm(tokens, norm_gain):
    wide_tokens = tokens.astype(jnp.float32)
    row_scale = lax.rsqrt(jnp.mean(wide_tokens * wide_tokens, -1, keepdims=True) + 1e-05)
    return (wide_tokens * row_scale * norm_gain).astype(jnp.bfloat16)


def gather_ctx(x):
    for axis in GATHER_ORDER:
        x = lax.all_gather(x, axis, axis=0, tiled=True)
    return x


def to_gathered_order(x, sizes):
    nz, nxh, nc = sizes
    lead = x.shape[:-2]
    y = x.reshape(lead + (nz, nxh, nc, x.shape[-1]))
    n = len(lead)
    y = jnp.transpose(y, tuple(range(n)) + (n + 2, n + 1, n, n + 3))
    return y.reshape(x.shape)


def from_gathered_order(x, sizes):
    nz, nxh, nc = sizes
    lead = x.shape[:-2]
    y = x.reshape(lead + (nc, nxh, nz, x.shape[-1]))
    n = len(lead)
    y = jnp.transpose(y, tuple(range(n)) + (n + 2, n + 1, n, n + 3))
    return y.reshape(x.shape)


def make_local(sizes):
    nz, nxh, nc = sizes
    nctx = nz * nxh * nc

    def local(tokens, norm_gain, w_query, w_key, w_value, w_out, row_map, doc_lengths, doc_labels):
        tok_rows, width = tokens.shape
        d_rows = w_query.shape[0]
        q_cols = w_query.shape[1]
        kv_cols = w_key.shape[1]
        group_size = q_cols // kv_cols
        runs_here = tok_rows // RUN
        total_runs = runs_here * nctx
        win_runs = MOST // RUN + 1

        normed = rms_norm(tokens, norm_gain)
        doc_index, in_doc, doc_ends = doc_layout(row_map, doc_lengths)

        w_cols = q_cols + 2 * kv_cols + w_out.shape[0]
        pos_row = jnp.concatenate(
            [
                (row_map // RUN).astype(jnp.bfloat16),
                (row_map % RUN).astype(jnp.bfloat16),
                jnp.zeros((w_cols - 2 * tok_rows,), jnp.bfloat16),
            ]
        )[None, :]
        pad_rows = 8 - (d_rows + 1) % 8 if (d_rows + 1) % 8 else 0
        buf = jnp.concatenate(
            [
                jnp.concatenate([w_query, w_key, w_value, w_out.T], axis=1),
                pos_row,
                jnp.zeros((pad_rows, w_cols), jnp.bfloat16),
            ],
            axis=0,
        )
        blk_rows = buf.shape[0]
        gathered = gather_ctx(buf).reshape(nctx, blk_rows, w_cols)
        w_blocks = gathered[:, :d_rows, :]
        pos_code = gathered[:, d_rows, : 2 * tok_rows].astype(jnp.int32)
        key_pos_all = pos_code[:, :tok_rows] * RUN + pos_code[:, tok_rows:]

        normed_g = to_gathered_order(normed.reshape(tok_rows, nctx, d_rows), sizes)
        proj = jnp.einsum(
            "tjd,jdn->tn", normed_g, w_blocks[:, :, : q_cols + 2 * kv_cols],
            preferred_element_type=jnp.float32,
        )
        queries = proj[:, :q_cols].reshape(tok_rows, group_size, HEAD_DIM)
        key_proj = proj[:, q_cols : q_cols + kv_cols]
        value_proj = proj[:, q_cols + kv_cols :].astype(jnp.bfloat16)
        queries = rotate(queries, in_doc).astype(jnp.bfloat16)
        key_proj = rotate(key_proj, in_doc).astype(jnp.bfloat16)

        kv = gather_ctx(jnp.concatenate([key_proj, value_proj], axis=1))
        kv_halves = kv.reshape(total_runs, RUN, 2 * kv_cols)
        pos_halves = key_pos_all.reshape(total_runs, RUN)
        run_of_half = pos_halves[:, 0] // RUN
        half_of_run = jnp.zeros((total_runs,), jnp.int32).at[run_of_half].set(
            jnp.arange(total_runs, dtype=jnp.int32)
        )

        q_pos = row_map.reshape(runs_here, RUN)
        q_start = (row_map - in_doc).reshape(runs_here, RUN)
        q_run = q_pos[:, 0] // RUN
        first_run = jnp.maximum(q_run - (win_runs - 1), 0)
        win = first_run[:, None] + jnp.arange(win_runs, dtype=jnp.int32)[None, :]
        win_halves = half_of_run[win]
        kv_win = kv_halves[win_halves].reshape(runs_here, win_runs * RUN, 2 * kv_cols)
        k_pos = pos_halves[win_halves].reshape(runs_here, win_runs * RUN)
        k_win = kv_win[..., :kv_cols]
        v_win = kv_win[..., kv_cols:]

        q_runs = queries.reshape(runs_here, RUN, group_size, HEAD_DIM)
        scale_factor = HEAD_DIM ** (-0.5)
        scores = (
            jnp.einsum("rqgd,rkd->rgqk", q_runs, k_win, preferred_element_type=jnp.float32)
            * scale_factor
        )
        allowed = (k_pos[:, None, :] >= q_start[:, :, None]) & (k_pos[:, None, :] <= q_pos[:, :, None])
        allowed = allowed[:, None]
        scores = jnp.where(allowed, scores, NEG_FILL)
        row_top = jnp.max(scores, -1, keepdims=True)
        weights = jnp.where(allowed, jnp.exp(scores - row_top), 0.0)
        row_sum = jnp.sum(weights, -1, keepdims=True)
        mixed = (
            jnp.einsum(
                "rgqk,rkd->rgqd", weights.astype(jnp.bfloat16), v_win,
                preferred_element_type=jnp.float32,
            )
            / row_sum
        ).astype(jnp.bfloat16)
        attended = jnp.transpose(mixed, (0, 2, 1, 3)).reshape(tok_rows, q_cols)

        partial_g = jnp.einsum(
            "tk,jdk->tjd", attended, w_blocks[:, :, q_cols + 2 * kv_cols :],
            preferred_element_type=jnp.float32,
        )
        partial_out = from_gathered_order(partial_g, sizes).reshape(tok_rows, width)
        head_share = lax.psum_scatter(
            partial_out.astype(jnp.bfloat16), HEAD, scatter_dimension=1, tiled=True
        ).astype(jnp.float32)
        col_width = head_share.shape[1]
        head_idx = lax.axis_index("y") * lax.axis_size("xl") + lax.axis_index("xl")
        own_cols = lax.dynamic_slice_in_dim(tokens, head_idx * col_width, col_width, 1)
        residual_out = (own_cols.astype(jnp.float32) + head_share).astype(jnp.bfloat16)

        is_last = row_map[:, None] == (doc_ends - 1)[None, :]
        label_f = doc_labels.astype(jnp.float32)
        harmful = jnp.sum(label_f)
        harmless = doc_labels.shape[0] - jnp.sum(label_f)
        stream = residual_out.astype(jnp.float32)
        harm_rows = jnp.sum(jnp.where(is_last, label_f[None, :], 0.0), 1)
        safe_rows = jnp.sum(jnp.where(is_last, (1.0 - label_f)[None, :], 0.0), 1)
        sums = jnp.stack(
            [jnp.sum(harm_rows[:, None] * stream, 0), jnp.sum(safe_rows[:, None] * stream, 0)]
        )
        for axis in ("c", "xh", "z"):
            sums = lax.psum(sums, axis)
        refusal_direction = sums[0] / harmful - sums[1] / harmless
        return (residual_out, refusal_direction)

    return local


def solution(mesh):
    n_ctx = mesh.shape["ctx"]
    n_head = mesh.shape["head"]
    nc, nxh = 2, 2
    nz = n_ctx // (nc * nxh)
    ny, nxl = n_head // 2, 2
    fine = Mesh(mesh.devices.reshape(nz, nxh, nc, ny, nxl), ("z", "xh", "c", "y", "xl"))
    placed = (
        P(CTX, None),
        P(),
        P(CTX, HEAD),
        P(CTX, HEAD),
        P(CTX, HEAD),
        P(HEAD, CTX),
        P(CTX),
        P(),
        P(),
    )
    return jax.shard_map(
        make_local((nz, nxh, nc)),
        mesh=fine,
        in_specs=placed,
        out_specs=(P(CTX, HEAD), P(HEAD)),
        check_vma=False,
    )
```

```python
import math

import jax
import jax.numpy as jnp
from jax import lax
from jax.sharding import Mesh
from jax.sharding import PartitionSpec as P

HEADS = 32
KV_HEADS = 8
HEAD_DIM = 128
MOST = 2048
RUN = 64

ROPE_BASE = 500000.0
NEG_FILL = -1e30

CTX = ("z", "xh", "c")
HEAD = ("y", "xl")


def doc_layout(row_map, doc_lengths):
    doc_ends = jnp.cumsum(doc_lengths)
    doc_starts = doc_ends - doc_lengths
    doc_index = jnp.sum((row_map[:, None] >= doc_ends[None, :]).astype(jnp.int32), 1)
    member = doc_index[:, None] == jnp.arange(doc_ends.shape[0], dtype=jnp.int32)[None, :]
    in_doc = row_map - jnp.sum(jnp.where(member, doc_starts[None, :], 0), 1)
    return (doc_index, in_doc, doc_ends)


def rotate(values, in_doc):
    head_dim = values.shape[-1]
    half_dim = head_dim // 2
    inv_freq = jnp.exp(
        jnp.arange(half_dim).astype(jnp.float32) * (-2.0 * math.log(ROPE_BASE) / head_dim)
    )
    angles = in_doc.astype(jnp.float32)[:, None] * inv_freq[None, :]
    shape_out = (angles.shape[0],) + (1,) * (values.ndim - 2) + (half_dim,)
    cosine = jnp.cos(angles).reshape(shape_out)
    sine_val = jnp.sin(angles).reshape(shape_out)
    front_half = values[..., :half_dim]
    back_half = values[..., half_dim:]
    return jnp.concatenate(
        [front_half * cosine - back_half * sine_val, back_half * cosine + front_half * sine_val], -1
    )


def rms_norm(tokens, norm_gain):
    wide_tokens = tokens.astype(jnp.float32)
    row_scale = lax.rsqrt(jnp.mean(wide_tokens * wide_tokens, -1, keepdims=True) + 1e-05)
    return (wide_tokens * row_scale * norm_gain).astype(jnp.bfloat16)


def swap_cat(x, axis_name):
    return jnp.concatenate([x, lax.ppermute(x, axis_name, [(0, 1), (1, 0)])], 0)


def gather_ctx(x):
    x = lax.all_gather(x, "z", axis=0, tiled=True)
    x = swap_cat(x, "xh")
    return swap_cat(x, "c")


def relative_index():
    return (
        lax.axis_index("c") ^ jnp.arange(2, dtype=jnp.int32),
        lax.axis_index("xh") ^ jnp.arange(2, dtype=jnp.int32),
    )


def to_gathered_order(x, sizes):
    nz, nxh, nc = sizes
    c_idx, xh_idx = relative_index()
    y = jnp.transpose(x.reshape(x.shape[0], nz, nxh, nc, x.shape[-1]), (0, 3, 2, 1, 4))
    y = jnp.take(jnp.take(y, c_idx, axis=1), xh_idx, axis=2)
    return y.reshape(x.shape)


def from_gathered_order(x, sizes):
    nz, nxh, nc = sizes
    c_idx, xh_idx = relative_index()
    y = x.reshape(x.shape[0], nc, nxh, nz, x.shape[-1])
    y = jnp.take(jnp.take(y, c_idx, axis=1), xh_idx, axis=2)
    return jnp.transpose(y, (0, 3, 2, 1, 4)).reshape(x.shape)


def make_local(sizes):
    nz, nxh, nc = sizes
    nctx = nz * nxh * nc

    def local(tokens, norm_gain, w_query, w_key, w_value, w_out, row_map, doc_lengths, doc_labels):
        tok_rows, width = tokens.shape
        d_rows = w_query.shape[0]
        q_cols = w_query.shape[1]
        kv_cols = w_key.shape[1]
        group_size = q_cols // kv_cols
        runs_here = tok_rows // RUN
        total_runs = runs_here * nctx
        win_runs = MOST // RUN + 1

        normed = rms_norm(tokens, norm_gain)
        doc_index, in_doc, doc_ends = doc_layout(row_map, doc_lengths)

        qkv_cols = q_cols + 2 * kv_cols
        pos_row = jnp.concatenate(
            [
                (row_map // RUN).astype(jnp.bfloat16),
                (row_map % RUN).astype(jnp.bfloat16),
                jnp.zeros((qkv_cols - 2 * tok_rows,), jnp.bfloat16),
            ]
        )[None, :]
        pad_rows = -(d_rows + 1) % 8
        buf = jnp.concatenate(
            [
                jnp.concatenate([w_query, w_key, w_value], axis=1),
                pos_row,
                jnp.zeros((pad_rows, qkv_cols), jnp.bfloat16),
            ],
            axis=0,
        )
        blk_rows = buf.shape[0]
        w_qkv = gather_ctx(buf).reshape(nctx, blk_rows, qkv_cols)
        w_o = gather_ctx(w_out.T).reshape(nctx, d_rows, w_out.shape[0])
        pos_code = w_qkv[:, d_rows, : 2 * tok_rows].astype(jnp.int32)
        key_pos_all = pos_code[:, :tok_rows] * RUN + pos_code[:, tok_rows:]

        normed_g = to_gathered_order(normed.reshape(tok_rows, nctx, d_rows), sizes)
        normed_g = jnp.pad(normed_g, ((0, 0), (0, 0), (0, blk_rows - d_rows)))
        proj = jnp.einsum(
            "tjd,jdn->tn", normed_g, w_qkv, preferred_element_type=jnp.float32,
        )
        queries = proj[:, :q_cols].reshape(tok_rows, group_size, HEAD_DIM)
        key_proj = proj[:, q_cols : q_cols + kv_cols]
        value_proj = proj[:, q_cols + kv_cols :].astype(jnp.bfloat16)
        queries = rotate(queries, in_doc).astype(jnp.bfloat16)
        key_proj = rotate(key_proj, in_doc).astype(jnp.bfloat16)

        kv = gather_ctx(jnp.concatenate([key_proj, value_proj], axis=1))
        kv_halves = kv.reshape(total_runs, RUN, 2 * kv_cols)
        pos_halves = key_pos_all.reshape(total_runs, RUN)
        run_of_half = pos_halves[:, 0] // RUN
        half_of_run = jnp.zeros((total_runs,), jnp.int32).at[run_of_half].set(
            jnp.arange(total_runs, dtype=jnp.int32)
        )

        q_pos = row_map.reshape(runs_here, RUN)
        q_start = (row_map - in_doc).reshape(runs_here, RUN)
        q_run = q_pos[:, 0] // RUN
        first_run = jnp.maximum(q_run - (win_runs - 1), 0)
        win = first_run[:, None] + jnp.arange(win_runs, dtype=jnp.int32)[None, :]
        win_halves = half_of_run[win]
        kv_win = kv_halves[win_halves].reshape(runs_here, win_runs * RUN, 2 * kv_cols)
        k_pos = pos_halves[win_halves].reshape(runs_here, win_runs * RUN)
        k_win = kv_win[..., :kv_cols]
        v_win = kv_win[..., kv_cols:]

        q_runs = queries.reshape(runs_here, RUN, group_size, HEAD_DIM)
        scale_factor = HEAD_DIM ** (-0.5)
        scores = (
            jnp.einsum("rqgd,rkd->rgqk", q_runs, k_win, preferred_element_type=jnp.float32)
            * scale_factor
        )
        allowed = (k_pos[:, None, :] >= q_start[:, :, None]) & (k_pos[:, None, :] <= q_pos[:, :, None])
        allowed = allowed[:, None]
        scores = jnp.where(allowed, scores, NEG_FILL)
        row_top = jnp.max(scores, -1, keepdims=True)
        weights = jnp.where(allowed, jnp.exp(scores - row_top), 0.0)
        row_sum = jnp.sum(weights, -1, keepdims=True)
        mixed = (
            jnp.einsum(
                "rgqk,rkd->rgqd", weights.astype(jnp.bfloat16), v_win,
                preferred_element_type=jnp.float32,
            )
            / row_sum
        ).astype(jnp.bfloat16)
        attended = jnp.transpose(mixed, (0, 2, 1, 3)).reshape(tok_rows, q_cols)

        partial_g = jnp.einsum(
            "tk,jdk->tjd", attended, w_o,
            preferred_element_type=jnp.float32,
        )
        partial_out = from_gathered_order(partial_g, sizes).reshape(tok_rows, width)
        head_share = lax.psum_scatter(
            partial_out.astype(jnp.bfloat16), HEAD, scatter_dimension=1, tiled=True
        ).astype(jnp.float32)
        col_width = head_share.shape[1]
        head_idx = lax.axis_index("y") * lax.axis_size("xl") + lax.axis_index("xl")
        own_cols = lax.dynamic_slice_in_dim(tokens, head_idx * col_width, col_width, 1)
        residual_out = (own_cols.astype(jnp.float32) + head_share).astype(jnp.bfloat16)

        is_last = row_map[:, None] == (doc_ends - 1)[None, :]
        label_f = doc_labels.astype(jnp.float32)
        harmful = jnp.sum(label_f)
        harmless = doc_labels.shape[0] - jnp.sum(label_f)
        stream = residual_out.astype(jnp.float32)
        harm_rows = jnp.sum(jnp.where(is_last, label_f[None, :], 0.0), 1)
        safe_rows = jnp.sum(jnp.where(is_last, (1.0 - label_f)[None, :], 0.0), 1)
        sums = jnp.stack(
            [jnp.sum(harm_rows[:, None] * stream, 0), jnp.sum(safe_rows[:, None] * stream, 0)]
        )
        for axis in ("c", "xh", "z"):
            sums = lax.psum(sums, axis)
        refusal_direction = sums[0] / harmful - sums[1] / harmless
        return (residual_out, refusal_direction)

    return local


def solution(mesh):
    n_ctx = mesh.shape["ctx"]
    n_head = mesh.shape["head"]
    nc, nxh = 2, 2
    nz = n_ctx // (nc * nxh)
    ny, nxl = n_head // 2, 2
    fine = Mesh(mesh.devices.reshape(nz, nxh, nc, ny, nxl), ("z", "xh", "c", "y", "xl"))
    placed = (
        P(CTX, None),
        P(),
        P(CTX, HEAD),
        P(CTX, HEAD),
        P(CTX, HEAD),
        P(HEAD, CTX),
        P(CTX),
        P(),
        P(),
    )
    return jax.shard_map(
        make_local((nz, nxh, nc)),
        mesh=fine,
        in_specs=placed,
        out_specs=(P(CTX, HEAD), P(HEAD)),
        check_vma=False,
    )
```

```python
import math

import jax
import jax.numpy as jnp
from jax import lax
from jax.sharding import Mesh
from jax.sharding import PartitionSpec as P

HEADS = 32
KV_HEADS = 8
HEAD_DIM = 128
MOST = 2048
RUN = 64

ROPE_BASE = 500000.0
NEG_FILL = -1e30

CTX = ("z", "xh", "c")
HEAD = ("y", "xl")


def doc_layout(row_map, doc_lengths):
    doc_ends = jnp.cumsum(doc_lengths)
    doc_starts = doc_ends - doc_lengths
    doc_index = jnp.sum((row_map[:, None] >= doc_ends[None, :]).astype(jnp.int32), 1)
    member = doc_index[:, None] == jnp.arange(doc_ends.shape[0], dtype=jnp.int32)[None, :]
    in_doc = row_map - jnp.sum(jnp.where(member, doc_starts[None, :], 0), 1)
    return (doc_index, in_doc, doc_ends)


def rotate(values, in_doc):
    head_dim = values.shape[-1]
    half_dim = head_dim // 2
    inv_freq = jnp.exp(
        jnp.arange(half_dim).astype(jnp.float32) * (-2.0 * math.log(ROPE_BASE) / head_dim)
    )
    angles = in_doc.astype(jnp.float32)[:, None] * inv_freq[None, :]
    shape_out = (angles.shape[0],) + (1,) * (values.ndim - 2) + (half_dim,)
    cosine = jnp.cos(angles).reshape(shape_out)
    sine_val = jnp.sin(angles).reshape(shape_out)
    front_half = values[..., :half_dim]
    back_half = values[..., half_dim:]
    return jnp.concatenate(
        [front_half * cosine - back_half * sine_val, back_half * cosine + front_half * sine_val], -1
    )


def rms_norm(tokens, norm_gain):
    wide_tokens = tokens.astype(jnp.float32)
    row_scale = lax.rsqrt(jnp.mean(wide_tokens * wide_tokens, -1, keepdims=True) + 1e-05)
    return (wide_tokens * row_scale * norm_gain).astype(jnp.bfloat16)


def swap_cat(x, axis_name):
    return jnp.concatenate([x, lax.ppermute(x, axis_name, [(0, 1), (1, 0)])], 0)


def gather_z(x):
    return lax.all_gather(x, "z", axis=0, tiled=True)


def gather_pair(x):
    return swap_cat(swap_cat(x, "xh"), "c")


def relative_index():
    return (
        lax.axis_index("c") ^ jnp.arange(2, dtype=jnp.int32),
        lax.axis_index("xh") ^ jnp.arange(2, dtype=jnp.int32),
    )


def to_gathered_order(x, sizes):
    nz, nxh, nc = sizes
    c_idx, xh_idx = relative_index()
    y = jnp.transpose(x.reshape(x.shape[0], nz, nxh, nc, x.shape[-1]), (0, 3, 2, 1, 4))
    y = jnp.take(jnp.take(y, c_idx, axis=1), xh_idx, axis=2)
    return y.reshape(x.shape)


def from_gathered_order(x, sizes):
    nz, nxh, nc = sizes
    c_idx, xh_idx = relative_index()
    y = x.reshape(x.shape[0], nc, nxh, nz, x.shape[-1])
    y = jnp.take(jnp.take(y, c_idx, axis=1), xh_idx, axis=2)
    return jnp.transpose(y, (0, 3, 2, 1, 4)).reshape(x.shape)


def make_local(sizes):
    nz, nxh, nc = sizes
    nctx = nz * nxh * nc

    def local(tokens, norm_gain, w_query, w_key, w_value, w_out, row_map, doc_lengths, doc_labels):
        tok_rows, width = tokens.shape
        d_rows = w_query.shape[0]
        q_cols = w_query.shape[1]
        kv_cols = w_key.shape[1]
        group_size = q_cols // kv_cols
        runs_here = tok_rows // RUN
        total_runs = runs_here * nctx
        win_runs = MOST // RUN + 1

        normed = rms_norm(tokens, norm_gain)
        doc_index, in_doc, doc_ends = doc_layout(row_map, doc_lengths)

        qkv_cols = q_cols + 2 * kv_cols
        pos_row = jnp.concatenate(
            [
                (row_map // RUN).astype(jnp.bfloat16),
                (row_map % RUN).astype(jnp.bfloat16),
                jnp.zeros((qkv_cols - 2 * tok_rows,), jnp.bfloat16),
            ]
        )[None, :]
        pad_rows = -(d_rows + 1) % 8
        out_cols = w_out.shape[0]
        buf = jnp.concatenate(
            [
                jnp.concatenate([w_query, w_key, w_value, w_out.T], axis=1),
                jnp.pad(pos_row, ((0, pad_rows), (0, out_cols))),
            ],
            axis=0,
        )
        blk_rows = buf.shape[0]
        w_z = gather_z(buf)
        w_qkv = gather_pair(w_z[:, :qkv_cols]).reshape(nctx, blk_rows, qkv_cols)
        w_o = gather_pair(w_z[:, qkv_cols:]).reshape(nctx, blk_rows, out_cols)[:, :d_rows]
        pos_code = w_qkv[:, d_rows, : 2 * tok_rows].astype(jnp.int32)
        key_pos_all = pos_code[:, :tok_rows] * RUN + pos_code[:, tok_rows:]

        normed_g = to_gathered_order(normed.reshape(tok_rows, nctx, d_rows), sizes)
        normed_g = jnp.pad(normed_g, ((0, 0), (0, 0), (0, blk_rows - d_rows)))
        proj = jnp.einsum(
            "tjd,jdn->tn", normed_g, w_qkv, preferred_element_type=jnp.float32,
        )
        queries = proj[:, :q_cols].reshape(tok_rows, group_size, HEAD_DIM)
        key_proj = proj[:, q_cols : q_cols + kv_cols]
        value_proj = proj[:, q_cols + kv_cols :].astype(jnp.bfloat16)
        queries = rotate(queries, in_doc).astype(jnp.bfloat16)
        key_proj = rotate(key_proj, in_doc).astype(jnp.bfloat16)

        kv = gather_pair(gather_z(jnp.concatenate([key_proj, value_proj], axis=1)))
        kv_halves = kv.reshape(total_runs, RUN, 2 * kv_cols)
        pos_halves = key_pos_all.reshape(total_runs, RUN)
        run_of_half = pos_halves[:, 0] // RUN
        half_of_run = jnp.zeros((total_runs,), jnp.int32).at[run_of_half].set(
            jnp.arange(total_runs, dtype=jnp.int32)
        )

        q_pos = row_map.reshape(runs_here, RUN)
        q_start = (row_map - in_doc).reshape(runs_here, RUN)
        q_run = q_pos[:, 0] // RUN
        first_run = jnp.maximum(q_run - (win_runs - 1), 0)
        win = first_run[:, None] + jnp.arange(win_runs, dtype=jnp.int32)[None, :]
        win_halves = half_of_run[win]
        kv_win = kv_halves[win_halves].reshape(runs_here, win_runs * RUN, 2 * kv_cols)
        k_pos = pos_halves[win_halves].reshape(runs_here, win_runs * RUN)
        k_win = kv_win[..., :kv_cols]
        v_win = kv_win[..., kv_cols:]

        q_runs = queries.reshape(runs_here, RUN, group_size, HEAD_DIM)
        scale_factor = HEAD_DIM ** (-0.5)
        scores = (
            jnp.einsum("rqgd,rkd->rgqk", q_runs, k_win, preferred_element_type=jnp.float32)
            * scale_factor
        )
        allowed = (k_pos[:, None, :] >= q_start[:, :, None]) & (k_pos[:, None, :] <= q_pos[:, :, None])
        allowed = allowed[:, None]
        scores = jnp.where(allowed, scores, NEG_FILL)
        row_top = jnp.max(scores, -1, keepdims=True)
        weights = jnp.where(allowed, jnp.exp(scores - row_top), 0.0)
        row_sum = jnp.sum(weights, -1, keepdims=True)
        mixed = (
            jnp.einsum(
                "rgqk,rkd->rgqd", weights.astype(jnp.bfloat16), v_win,
                preferred_element_type=jnp.float32,
            )
            / row_sum
        ).astype(jnp.bfloat16)
        attended = jnp.transpose(mixed, (0, 2, 1, 3)).reshape(tok_rows, q_cols)

        partial_g = jnp.einsum(
            "tk,jdk->tjd", attended, w_o,
            preferred_element_type=jnp.float32,
        )
        partial_out = from_gathered_order(partial_g, sizes).reshape(tok_rows, width)
        head_share = lax.psum_scatter(
            partial_out.astype(jnp.bfloat16), HEAD, scatter_dimension=1, tiled=True
        ).astype(jnp.float32)
        col_width = head_share.shape[1]
        head_idx = lax.axis_index("y") * lax.axis_size("xl") + lax.axis_index("xl")
        own_cols = lax.dynamic_slice_in_dim(tokens, head_idx * col_width, col_width, 1)
        residual_out = (own_cols.astype(jnp.float32) + head_share).astype(jnp.bfloat16)

        is_last = row_map[:, None] == (doc_ends - 1)[None, :]
        label_f = doc_labels.astype(jnp.float32)
        harmful = jnp.sum(label_f)
        harmless = doc_labels.shape[0] - jnp.sum(label_f)
        stream = residual_out.astype(jnp.float32)
        harm_rows = jnp.sum(jnp.where(is_last, label_f[None, :], 0.0), 1)
        safe_rows = jnp.sum(jnp.where(is_last, (1.0 - label_f)[None, :], 0.0), 1)
        sums = jnp.stack(
            [jnp.sum(harm_rows[:, None] * stream, 0), jnp.sum(safe_rows[:, None] * stream, 0)]
        )
        for axis in ("c", "xh", "z"):
            sums = lax.psum(sums, axis)
        refusal_direction = sums[0] / harmful - sums[1] / harmless
        return (residual_out, refusal_direction)

    return local


def solution(mesh):
    n_ctx = mesh.shape["ctx"]
    n_head = mesh.shape["head"]
    nc, nxh = 2, 2
    nz = n_ctx // (nc * nxh)
    ny, nxl = n_head // 2, 2
    fine = Mesh(mesh.devices.reshape(nz, nxh, nc, ny, nxl), ("z", "xh", "c", "y", "xl"))
    placed = (
        P(CTX, None),
        P(),
        P(CTX, HEAD),
        P(CTX, HEAD),
        P(CTX, HEAD),
        P(HEAD, CTX),
        P(CTX),
        P(),
        P(),
    )
    return jax.shard_map(
        make_local((nz, nxh, nc)),
        mesh=fine,
        in_specs=placed,
        out_specs=(P(CTX, HEAD), P(HEAD)),
        check_vma=False,
    )
```

```python
import math

import jax
import jax.numpy as jnp
from jax import lax
from jax.sharding import Mesh
from jax.sharding import PartitionSpec as P

HEADS = 32
KV_HEADS = 8
HEAD_DIM = 128
MOST = 2048
RUN = 64

ROPE_BASE = 500000.0
NEG_FILL = -1e30

CTX = ("z", "xh", "c")
HEAD = ("y", "xl")


def doc_layout(row_map, doc_lengths):
    doc_ends = jnp.cumsum(doc_lengths)
    doc_starts = doc_ends - doc_lengths
    doc_index = jnp.sum((row_map[:, None] >= doc_ends[None, :]).astype(jnp.int32), 1)
    member = doc_index[:, None] == jnp.arange(doc_ends.shape[0], dtype=jnp.int32)[None, :]
    in_doc = row_map - jnp.sum(jnp.where(member, doc_starts[None, :], 0), 1)
    return (doc_index, in_doc, doc_ends)


def rotate(values, in_doc):
    head_dim = values.shape[-1]
    half_dim = head_dim // 2
    inv_freq = jnp.exp(
        jnp.arange(half_dim).astype(jnp.float32) * (-2.0 * math.log(ROPE_BASE) / head_dim)
    )
    angles = in_doc.astype(jnp.float32)[:, None] * inv_freq[None, :]
    shape_out = (angles.shape[0],) + (1,) * (values.ndim - 2) + (half_dim,)
    cosine = jnp.cos(angles).reshape(shape_out)
    sine_val = jnp.sin(angles).reshape(shape_out)
    front_half = values[..., :half_dim]
    back_half = values[..., half_dim:]
    return jnp.concatenate(
        [front_half * cosine - back_half * sine_val, back_half * cosine + front_half * sine_val], -1
    )


def rms_norm(tokens, norm_gain):
    wide_tokens = tokens.astype(jnp.float32)
    row_scale = lax.rsqrt(jnp.mean(wide_tokens * wide_tokens, -1, keepdims=True) + 1e-05)
    return (wide_tokens * row_scale * norm_gain).astype(jnp.bfloat16)


def swap_cat(x, axis_name):
    return jnp.concatenate([x, lax.ppermute(x, axis_name, [(0, 1), (1, 0)])], 0)


def gather_z(x):
    return lax.all_gather(x, "z", axis=0, tiled=True)


def gather_pair(x):
    return swap_cat(swap_cat(x, "xh"), "c")


def relative_index():
    return (
        lax.axis_index("c") ^ jnp.arange(2, dtype=jnp.int32),
        lax.axis_index("xh") ^ jnp.arange(2, dtype=jnp.int32),
    )


def to_gathered_order(x, sizes):
    nz, nxh, nc = sizes
    c_idx, xh_idx = relative_index()
    y = jnp.transpose(x.reshape(x.shape[0], nz, nxh, nc, x.shape[-1]), (0, 3, 2, 1, 4))
    y = jnp.take(jnp.take(y, c_idx, axis=1), xh_idx, axis=2)
    return y.reshape(x.shape)


def from_gathered_order(x, sizes):
    nz, nxh, nc = sizes
    c_idx, xh_idx = relative_index()
    y = x.reshape(x.shape[0], nc, nxh, nz, x.shape[-1])
    y = jnp.take(jnp.take(y, c_idx, axis=1), xh_idx, axis=2)
    return jnp.transpose(y, (0, 3, 2, 1, 4)).reshape(x.shape)


def reduce_scatter_head(x, head_sizes):
    ny, nxl = head_sizes
    rows, width = x.shape
    xl = lax.axis_index("xl")
    y = lax.axis_index("y")
    grouped = x.reshape(rows, ny, nxl, width // (ny * nxl))
    kept = jnp.take(grouped, xl, axis=2)
    sent = jnp.take(grouped, (xl + 1) % nxl, axis=2).astype(jnp.bfloat16)
    summed = kept + lax.ppermute(sent, "xl", [(0, 1), (1, 0)]).astype(jnp.float32)
    acc = jnp.take(summed, y, axis=1)
    for shift in range(1, ny):
        piece = jnp.take(summed, (y + shift) % ny, axis=1).astype(jnp.bfloat16)
        acc = acc + lax.ppermute(
            piece, "y", [(i, (i + shift) % ny) for i in range(ny)]
        ).astype(jnp.float32)
    return acc


def make_local(sizes, head_sizes):
    nz, nxh, nc = sizes
    nctx = nz * nxh * nc

    def local(tokens, norm_gain, w_query, w_key, w_value, w_out, row_map, doc_lengths, doc_labels):
        tok_rows, width = tokens.shape
        d_rows = w_query.shape[0]
        q_cols = w_query.shape[1]
        kv_cols = w_key.shape[1]
        group_size = q_cols // kv_cols
        runs_here = tok_rows // RUN
        total_runs = runs_here * nctx
        win_runs = MOST // RUN + 1

        normed = rms_norm(tokens, norm_gain)
        doc_index, in_doc, doc_ends = doc_layout(row_map, doc_lengths)

        qkv_cols = q_cols + 2 * kv_cols
        pos_row = jnp.concatenate(
            [
                (row_map // RUN).astype(jnp.bfloat16),
                (row_map % RUN).astype(jnp.bfloat16),
                jnp.zeros((qkv_cols - 2 * tok_rows,), jnp.bfloat16),
            ]
        )[None, :]
        pad_rows = -(d_rows + 1) % 8
        out_cols = w_out.shape[0]
        buf = jnp.concatenate(
            [
                jnp.concatenate([w_query, w_key, w_value, w_out.T], axis=1),
                jnp.pad(pos_row, ((0, pad_rows), (0, out_cols))),
            ],
            axis=0,
        )
        blk_rows = buf.shape[0]
        w_z = gather_z(buf)
        w_qkv = gather_pair(w_z[:, :qkv_cols]).reshape(nctx, blk_rows, qkv_cols)
        w_o = gather_pair(w_z[:, qkv_cols:]).reshape(nctx, blk_rows, out_cols)[:, :d_rows]
        pos_code = w_qkv[:, d_rows, : 2 * tok_rows].astype(jnp.int32)
        key_pos_all = pos_code[:, :tok_rows] * RUN + pos_code[:, tok_rows:]

        normed_g = to_gathered_order(normed.reshape(tok_rows, nctx, d_rows), sizes)
        normed_g = jnp.pad(normed_g, ((0, 0), (0, 0), (0, blk_rows - d_rows)))
        proj = jnp.einsum(
            "tjd,jdn->tn", normed_g, w_qkv, preferred_element_type=jnp.float32,
        )
        queries = proj[:, :q_cols].reshape(tok_rows, group_size, HEAD_DIM)
        key_proj = proj[:, q_cols : q_cols + kv_cols]
        value_proj = proj[:, q_cols + kv_cols :].astype(jnp.bfloat16)
        queries = rotate(queries, in_doc).astype(jnp.bfloat16)
        key_proj = rotate(key_proj, in_doc).astype(jnp.bfloat16)

        kv = gather_pair(gather_z(jnp.concatenate([key_proj, value_proj], axis=1)))
        kv_halves = kv.reshape(total_runs, RUN, 2 * kv_cols)
        pos_halves = key_pos_all.reshape(total_runs, RUN)
        run_of_half = pos_halves[:, 0] // RUN
        half_of_run = jnp.zeros((total_runs,), jnp.int32).at[run_of_half].set(
            jnp.arange(total_runs, dtype=jnp.int32)
        )

        q_pos = row_map.reshape(runs_here, RUN)
        q_start = (row_map - in_doc).reshape(runs_here, RUN)
        q_run = q_pos[:, 0] // RUN
        first_run = jnp.maximum(q_run - (win_runs - 1), 0)
        win = first_run[:, None] + jnp.arange(win_runs, dtype=jnp.int32)[None, :]
        win_halves = half_of_run[win]
        kv_win = kv_halves[win_halves].reshape(runs_here, win_runs * RUN, 2 * kv_cols)
        k_pos = pos_halves[win_halves].reshape(runs_here, win_runs * RUN)
        k_win = kv_win[..., :kv_cols]
        v_win = kv_win[..., kv_cols:]

        q_runs = queries.reshape(runs_here, RUN, group_size, HEAD_DIM)
        scale_factor = HEAD_DIM ** (-0.5)
        scores = (
            jnp.einsum("rqgd,rkd->rgqk", q_runs, k_win, preferred_element_type=jnp.float32)
            * scale_factor
        )
        allowed = (k_pos[:, None, :] >= q_start[:, :, None]) & (k_pos[:, None, :] <= q_pos[:, :, None])
        allowed = allowed[:, None]
        scores = jnp.where(allowed, scores, NEG_FILL)
        row_top = jnp.max(scores, -1, keepdims=True)
        weights = jnp.where(allowed, jnp.exp(scores - row_top), 0.0)
        row_sum = jnp.sum(weights, -1, keepdims=True)
        mixed = (
            jnp.einsum(
                "rgqk,rkd->rgqd", weights.astype(jnp.bfloat16), v_win,
                preferred_element_type=jnp.float32,
            )
            / row_sum
        ).astype(jnp.bfloat16)
        attended = jnp.transpose(mixed, (0, 2, 1, 3)).reshape(tok_rows, q_cols)

        partial_g = jnp.einsum(
            "tk,jdk->tjd", attended, w_o,
            preferred_element_type=jnp.float32,
        )
        partial_out = from_gathered_order(partial_g, sizes).reshape(tok_rows, width)
        head_share = reduce_scatter_head(partial_out, head_sizes)
        col_width = head_share.shape[1]
        head_idx = lax.axis_index("y") * head_sizes[1] + lax.axis_index("xl")
        own_cols = lax.dynamic_slice_in_dim(tokens, head_idx * col_width, col_width, 1)
        residual_out = (own_cols.astype(jnp.float32) + head_share).astype(jnp.bfloat16)

        is_last = row_map[:, None] == (doc_ends - 1)[None, :]
        label_f = doc_labels.astype(jnp.float32)
        harmful = jnp.sum(label_f)
        harmless = doc_labels.shape[0] - jnp.sum(label_f)
        stream = residual_out.astype(jnp.float32)
        harm_rows = jnp.sum(jnp.where(is_last, label_f[None, :], 0.0), 1)
        safe_rows = jnp.sum(jnp.where(is_last, (1.0 - label_f)[None, :], 0.0), 1)
        sums = jnp.stack(
            [jnp.sum(harm_rows[:, None] * stream, 0), jnp.sum(safe_rows[:, None] * stream, 0)]
        )
        for axis in ("c", "xh", "z"):
            sums = lax.psum(sums, axis)
        refusal_direction = sums[0] / harmful - sums[1] / harmless
        return (residual_out, refusal_direction)

    return local


def solution(mesh):
    n_ctx = mesh.shape["ctx"]
    n_head = mesh.shape["head"]
    nc, nxh = 2, 2
    nz = n_ctx // (nc * nxh)
    ny, nxl = n_head // 2, 2
    fine = Mesh(mesh.devices.reshape(nz, nxh, nc, ny, nxl), ("z", "xh", "c", "y", "xl"))
    placed = (
        P(CTX, None),
        P(),
        P(CTX, HEAD),
        P(CTX, HEAD),
        P(CTX, HEAD),
        P(HEAD, CTX),
        P(CTX),
        P(),
        P(),
    )
    return jax.shard_map(
        make_local((nz, nxh, nc), (ny, nxl)),
        mesh=fine,
        in_specs=placed,
        out_specs=(P(CTX, HEAD), P(HEAD)),
        check_vma=False,
    )
```

```python
import math

import jax
import jax.numpy as jnp
from jax import lax
from jax.sharding import Mesh
from jax.sharding import PartitionSpec as P

HEADS = 32
KV_HEADS = 8
HEAD_DIM = 128
MOST = 2048
RUN = 64

ROPE_BASE = 500000.0
NEG_FILL = -1e30

CTX = ("z", "xh", "c")
HEAD = ("y", "xl")


def doc_layout(row_map, doc_lengths):
    doc_ends = jnp.cumsum(doc_lengths)
    doc_starts = doc_ends - doc_lengths
    doc_index = jnp.sum((row_map[:, None] >= doc_ends[None, :]).astype(jnp.int32), 1)
    member = doc_index[:, None] == jnp.arange(doc_ends.shape[0], dtype=jnp.int32)[None, :]
    in_doc = row_map - jnp.sum(jnp.where(member, doc_starts[None, :], 0), 1)
    return (doc_index, in_doc, doc_ends)


def rotate(values, in_doc):
    head_dim = values.shape[-1]
    half_dim = head_dim // 2
    inv_freq = jnp.exp(
        jnp.arange(half_dim).astype(jnp.float32) * (-2.0 * math.log(ROPE_BASE) / head_dim)
    )
    angles = in_doc.astype(jnp.float32)[:, None] * inv_freq[None, :]
    shape_out = (angles.shape[0],) + (1,) * (values.ndim - 2) + (half_dim,)
    cosine = jnp.cos(angles).reshape(shape_out)
    sine_val = jnp.sin(angles).reshape(shape_out)
    front_half = values[..., :half_dim]
    back_half = values[..., half_dim:]
    return jnp.concatenate(
        [front_half * cosine - back_half * sine_val, back_half * cosine + front_half * sine_val], -1
    )


def rms_norm(tokens, norm_gain):
    wide_tokens = tokens.astype(jnp.float32)
    row_scale = lax.rsqrt(jnp.mean(wide_tokens * wide_tokens, -1, keepdims=True) + 1e-05)
    return (wide_tokens * row_scale * norm_gain).astype(jnp.bfloat16)


def swap_cat(x, axis_name):
    return jnp.concatenate([x, lax.ppermute(x, axis_name, [(0, 1), (1, 0)])], 0)


def gather_z(x):
    return lax.all_gather(x, "z", axis=0, tiled=True)


def gather_pair(x):
    return swap_cat(swap_cat(x, "xh"), "c")


def relative_index():
    return (
        lax.axis_index("c") ^ jnp.arange(2, dtype=jnp.int32),
        lax.axis_index("xh") ^ jnp.arange(2, dtype=jnp.int32),
    )


def to_gathered_order(x, sizes):
    nz, nxh, nc = sizes
    c_idx, xh_idx = relative_index()
    y = jnp.transpose(x.reshape(x.shape[0], nz, nxh, nc, x.shape[-1]), (0, 3, 2, 1, 4))
    y = jnp.take(jnp.take(y, c_idx, axis=1), xh_idx, axis=2)
    return y.reshape(x.shape)


def from_gathered_order(x, sizes):
    nz, nxh, nc = sizes
    c_idx, xh_idx = relative_index()
    y = x.reshape(x.shape[0], nc, nxh, nz, x.shape[-1])
    y = jnp.take(jnp.take(y, c_idx, axis=1), xh_idx, axis=2)
    return jnp.transpose(y, (0, 3, 2, 1, 4)).reshape(x.shape)


def reduce_scatter_head(x, head_sizes):
    ny, nxl = head_sizes
    rows, width = x.shape
    xl = lax.axis_index("xl")
    y = lax.axis_index("y")
    grouped = x.reshape(rows, ny, nxl, width // (ny * nxl))
    kept = jnp.take(grouped, xl, axis=2)
    sent = jnp.take(grouped, (xl + 1) % nxl, axis=2).astype(jnp.bfloat16)
    summed = kept + lax.ppermute(sent, "xl", [(0, 1), (1, 0)]).astype(jnp.float32)
    acc = jnp.take(summed, y, axis=1)
    for shift in range(1, ny):
        piece = jnp.take(summed, (y + shift) % ny, axis=1).astype(jnp.bfloat16)
        acc = acc + lax.ppermute(
            piece, "y", [(i, (i + shift) % ny) for i in range(ny)]
        ).astype(jnp.float32)
    return acc


def make_local(sizes, head_sizes):
    nz, nxh, nc = sizes
    nctx = nz * nxh * nc

    def local(tokens, norm_gain, w_query, w_key, w_value, w_out, row_map, doc_lengths, doc_labels):
        tok_rows, width = tokens.shape
        d_rows = w_query.shape[0]
        q_cols = w_query.shape[1]
        kv_cols = w_key.shape[1]
        group_size = q_cols // kv_cols
        runs_here = tok_rows // RUN
        total_runs = runs_here * nctx
        win_runs = MOST // RUN + 1

        normed = rms_norm(tokens, norm_gain)
        doc_index, in_doc, doc_ends = doc_layout(row_map, doc_lengths)

        qkv_cols = q_cols + 2 * kv_cols
        out_cols = w_out.shape[0]
        w_z = gather_z(jnp.concatenate([w_query, w_key, w_value, w_out.T], axis=1))
        w_o = gather_pair(w_z[:, qkv_cols:]).reshape(nctx, d_rows, out_cols)
        w_proj = w_z[:, :qkv_cols]

        pair = ("xh", "c")
        npair = nxh * nc
        me = lax.axis_index("xh") * nc + lax.axis_index("c")
        quarters = jnp.transpose(
            normed.reshape(tok_rows, nz, nxh, nc, d_rows), (0, 2, 3, 1, 4)
        ).reshape(tok_rows, npair, nz * d_rows)
        proj = jnp.dot(
            jnp.take(quarters, me, axis=1), w_proj, preferred_element_type=jnp.float32
        )
        for flip in range(1, npair):
            perm = [(i, i ^ flip) for i in range(npair)]
            theirs = lax.ppermute(jnp.take(quarters, me ^ flip, axis=1), pair, perm)
            part = jnp.dot(theirs, w_proj, preferred_element_type=jnp.float32)
            proj = proj + lax.ppermute(part, pair, perm)
        queries = proj[:, :q_cols].reshape(tok_rows, group_size, HEAD_DIM)
        key_proj = proj[:, q_cols : q_cols + kv_cols]
        value_proj = proj[:, q_cols + kv_cols :].astype(jnp.bfloat16)
        queries = rotate(queries, in_doc).astype(jnp.bfloat16)
        key_proj = rotate(key_proj, in_doc).astype(jnp.bfloat16)

        assert 2 * tok_rows == 2 * kv_cols
        pos_row = jnp.concatenate([row_map // RUN, row_map % RUN]).astype(jnp.bfloat16)[None, :]
        kv_buf = jnp.concatenate(
            [jnp.concatenate([key_proj, value_proj], axis=1), jnp.pad(pos_row, ((0, 7), (0, 0)))],
            axis=0,
        )
        kv = gather_pair(gather_z(kv_buf)).reshape(nctx, tok_rows + 8, 2 * kv_cols)
        pos_code = kv[:, tok_rows, :].astype(jnp.int32)
        key_pos_all = pos_code[:, :tok_rows] * RUN + pos_code[:, tok_rows:]
        kv_halves = kv[:, :tok_rows].reshape(total_runs, RUN, 2 * kv_cols)
        pos_halves = key_pos_all.reshape(total_runs, RUN)
        run_of_half = pos_halves[:, 0] // RUN
        half_of_run = jnp.zeros((total_runs,), jnp.int32).at[run_of_half].set(
            jnp.arange(total_runs, dtype=jnp.int32)
        )

        q_pos = row_map.reshape(runs_here, RUN)
        q_start = (row_map - in_doc).reshape(runs_here, RUN)
        q_run = q_pos[:, 0] // RUN
        first_run = jnp.maximum(q_run - (win_runs - 1), 0)
        win = first_run[:, None] + jnp.arange(win_runs, dtype=jnp.int32)[None, :]
        win_halves = half_of_run[win]
        kv_win = kv_halves[win_halves].reshape(runs_here, win_runs * RUN, 2 * kv_cols)
        k_pos = pos_halves[win_halves].reshape(runs_here, win_runs * RUN)
        k_win = kv_win[..., :kv_cols]
        v_win = kv_win[..., kv_cols:]

        q_runs = queries.reshape(runs_here, RUN, group_size, HEAD_DIM)
        scale_factor = HEAD_DIM ** (-0.5)
        scores = (
            jnp.einsum("rqgd,rkd->rgqk", q_runs, k_win, preferred_element_type=jnp.float32)
            * scale_factor
        )
        allowed = (k_pos[:, None, :] >= q_start[:, :, None]) & (k_pos[:, None, :] <= q_pos[:, :, None])
        allowed = allowed[:, None]
        scores = jnp.where(allowed, scores, NEG_FILL)
        row_top = jnp.max(scores, -1, keepdims=True)
        weights = jnp.where(allowed, jnp.exp(scores - row_top), 0.0)
        row_sum = jnp.sum(weights, -1, keepdims=True)
        mixed = (
            jnp.einsum(
                "rgqk,rkd->rgqd", weights.astype(jnp.bfloat16), v_win,
                preferred_element_type=jnp.float32,
            )
            / row_sum
        ).astype(jnp.bfloat16)
        attended = jnp.transpose(mixed, (0, 2, 1, 3)).reshape(tok_rows, q_cols)

        partial_g = jnp.einsum(
            "tk,jdk->tjd", attended, w_o,
            preferred_element_type=jnp.float32,
        )
        partial_out = from_gathered_order(partial_g, sizes).reshape(tok_rows, width)
        head_share = reduce_scatter_head(partial_out, head_sizes)
        col_width = head_share.shape[1]
        head_idx = lax.axis_index("y") * head_sizes[1] + lax.axis_index("xl")
        own_cols = lax.dynamic_slice_in_dim(tokens, head_idx * col_width, col_width, 1)
        residual_out = (own_cols.astype(jnp.float32) + head_share).astype(jnp.bfloat16)

        is_last = row_map[:, None] == (doc_ends - 1)[None, :]
        label_f = doc_labels.astype(jnp.float32)
        harmful = jnp.sum(label_f)
        harmless = doc_labels.shape[0] - jnp.sum(label_f)
        stream = residual_out.astype(jnp.float32)
        harm_rows = jnp.sum(jnp.where(is_last, label_f[None, :], 0.0), 1)
        safe_rows = jnp.sum(jnp.where(is_last, (1.0 - label_f)[None, :], 0.0), 1)
        sums = jnp.stack(
            [jnp.sum(harm_rows[:, None] * stream, 0), jnp.sum(safe_rows[:, None] * stream, 0)]
        )
        for axis in ("c", "xh", "z"):
            sums = lax.psum(sums, axis)
        refusal_direction = sums[0] / harmful - sums[1] / harmless
        return (residual_out, refusal_direction)

    return local


def solution(mesh):
    n_ctx = mesh.shape["ctx"]
    n_head = mesh.shape["head"]
    nc, nxh = 2, 2
    nz = n_ctx // (nc * nxh)
    ny, nxl = n_head // 2, 2
    fine = Mesh(mesh.devices.reshape(nz, nxh, nc, ny, nxl), ("z", "xh", "c", "y", "xl"))
    placed = (
        P(CTX, None),
        P(),
        P(CTX, HEAD),
        P(CTX, HEAD),
        P(CTX, HEAD),
        P(HEAD, CTX),
        P(CTX),
        P(),
        P(),
    )
    return jax.shard_map(
        make_local((nz, nxh, nc), (ny, nxl)),
        mesh=fine,
        in_specs=placed,
        out_specs=(P(CTX, HEAD), P(HEAD)),
        check_vma=False,
    )
```

```python
import math

import jax
import jax.numpy as jnp
from jax import lax
from jax.sharding import Mesh
from jax.sharding import PartitionSpec as P

HEADS = 32
KV_HEADS = 8
HEAD_DIM = 128
MOST = 2048
RUN = 64

ROPE_BASE = 500000.0
NEG_FILL = -1e30

CTX = ("z", "xh", "c")
HEAD = ("y", "xl")


def doc_layout(row_map, doc_lengths):
    doc_ends = jnp.cumsum(doc_lengths)
    doc_starts = doc_ends - doc_lengths
    doc_index = jnp.sum((row_map[:, None] >= doc_ends[None, :]).astype(jnp.int32), 1)
    member = doc_index[:, None] == jnp.arange(doc_ends.shape[0], dtype=jnp.int32)[None, :]
    in_doc = row_map - jnp.sum(jnp.where(member, doc_starts[None, :], 0), 1)
    return (doc_index, in_doc, doc_ends)


def rotate(values, in_doc):
    head_dim = values.shape[-1]
    half_dim = head_dim // 2
    inv_freq = jnp.exp(
        jnp.arange(half_dim).astype(jnp.float32) * (-2.0 * math.log(ROPE_BASE) / head_dim)
    )
    angles = in_doc.astype(jnp.float32)[:, None] * inv_freq[None, :]
    shape_out = (angles.shape[0],) + (1,) * (values.ndim - 2) + (half_dim,)
    cosine = jnp.cos(angles).reshape(shape_out)
    sine_val = jnp.sin(angles).reshape(shape_out)
    front_half = values[..., :half_dim]
    back_half = values[..., half_dim:]
    return jnp.concatenate(
        [front_half * cosine - back_half * sine_val, back_half * cosine + front_half * sine_val], -1
    )


def rms_norm(tokens, norm_gain):
    wide_tokens = tokens.astype(jnp.float32)
    row_scale = lax.rsqrt(jnp.mean(wide_tokens * wide_tokens, -1, keepdims=True) + 1e-05)
    return (wide_tokens * row_scale * norm_gain).astype(jnp.bfloat16)


def swap_cat(x, axis_name):
    return jnp.concatenate([x, lax.ppermute(x, axis_name, [(0, 1), (1, 0)])], 0)


def gather_z(x):
    return lax.all_gather(x, "z", axis=0, tiled=True)


def gather_pair(x):
    return swap_cat(swap_cat(x, "xh"), "c")


def relative_index():
    return (
        lax.axis_index("c") ^ jnp.arange(2, dtype=jnp.int32),
        lax.axis_index("xh") ^ jnp.arange(2, dtype=jnp.int32),
    )


def to_gathered_order(x, sizes):
    nz, nxh, nc = sizes
    c_idx, xh_idx = relative_index()
    y = jnp.transpose(x.reshape(x.shape[0], nz, nxh, nc, x.shape[-1]), (0, 3, 2, 1, 4))
    y = jnp.take(jnp.take(y, c_idx, axis=1), xh_idx, axis=2)
    return y.reshape(x.shape)


def from_gathered_order(x, sizes):
    nz, nxh, nc = sizes
    c_idx, xh_idx = relative_index()
    y = x.reshape(x.shape[0], nc, nxh, nz, x.shape[-1])
    y = jnp.take(jnp.take(y, c_idx, axis=1), xh_idx, axis=2)
    return jnp.transpose(y, (0, 3, 2, 1, 4)).reshape(x.shape)


def reduce_scatter_head(x, head_sizes):
    ny, nxl = head_sizes
    rows, width = x.shape
    xl = lax.axis_index("xl")
    y = lax.axis_index("y")
    grouped = x.reshape(rows, ny, nxl, width // (ny * nxl))
    kept = jnp.take(grouped, xl, axis=2)
    sent = jnp.take(grouped, (xl + 1) % nxl, axis=2).astype(jnp.bfloat16)
    summed = kept + lax.ppermute(sent, "xl", [(0, 1), (1, 0)]).astype(jnp.float32)
    acc = jnp.take(summed, y, axis=1)
    for shift in range(1, ny):
        piece = jnp.take(summed, (y + shift) % ny, axis=1).astype(jnp.bfloat16)
        acc = acc + lax.ppermute(
            piece, "y", [(i, (i + shift) % ny) for i in range(ny)]
        ).astype(jnp.float32)
    return acc


def make_local(sizes, head_sizes):
    nz, nxh, nc = sizes
    nctx = nz * nxh * nc

    def local(tokens, norm_gain, w_query, w_key, w_value, w_out, row_map, doc_lengths, doc_labels):
        tok_rows, width = tokens.shape
        d_rows = w_query.shape[0]
        q_cols = w_query.shape[1]
        kv_cols = w_key.shape[1]
        group_size = q_cols // kv_cols
        runs_here = tok_rows // RUN
        total_runs = runs_here * nctx
        win_runs = MOST // RUN + 1

        normed = rms_norm(tokens, norm_gain)
        doc_index, in_doc, doc_ends = doc_layout(row_map, doc_lengths)

        qkv_cols = q_cols + 2 * kv_cols
        out_cols = w_out.shape[0]
        w_z = gather_z(jnp.concatenate([w_query, w_key, w_value, w_out.T], axis=1))
        w_o = gather_pair(w_z[:, qkv_cols:]).reshape(nctx, d_rows, out_cols)
        w_proj = w_z[:, :qkv_cols]

        pair = ("xh", "c")
        npair = nxh * nc
        me = lax.axis_index("xh") * nc + lax.axis_index("c")
        quarters = jnp.transpose(
            normed.reshape(tok_rows, nz, nxh, nc, d_rows), (0, 2, 3, 1, 4)
        ).reshape(tok_rows, npair, nz * d_rows)
        proj = jnp.dot(
            jnp.take(quarters, me, axis=1), w_proj, preferred_element_type=jnp.float32
        )
        for flip in range(1, npair):
            perm = [(i, i ^ flip) for i in range(npair)]
            theirs = lax.ppermute(jnp.take(quarters, me ^ flip, axis=1), pair, perm)
            part = jnp.dot(theirs, w_proj, preferred_element_type=jnp.float32)
            proj = proj + lax.ppermute(part, pair, perm)
        queries = proj[:, :q_cols].reshape(tok_rows, group_size, HEAD_DIM)
        key_proj = proj[:, q_cols : q_cols + kv_cols]
        value_proj = proj[:, q_cols + kv_cols :].astype(jnp.bfloat16)
        queries = rotate(queries, in_doc).astype(jnp.bfloat16)
        key_proj = rotate(key_proj, in_doc).astype(jnp.bfloat16)

        assert 2 * tok_rows == 2 * kv_cols
        pos_row = jnp.concatenate([row_map // RUN, row_map % RUN]).astype(jnp.bfloat16)[None, :]
        kv_buf = jnp.concatenate(
            [jnp.concatenate([key_proj, value_proj], axis=1), jnp.pad(pos_row, ((0, 7), (0, 0)))],
            axis=0,
        )
        kv_z = gather_z(kv_buf)
        kv_zx = (kv_z, lax.ppermute(kv_z, "xh", [(0, 1), (1, 0)]))
        kv_pieces = kv_zx + tuple(lax.ppermute(kv_zx, "c", [(0, 1), (1, 0)]))
        blk_rows = tok_rows + 8
        pos_code = jnp.concatenate(
            [p.reshape(nz, blk_rows, 2 * kv_cols)[:, tok_rows, :] for p in kv_pieces]
        ).astype(jnp.int32)
        key_pos_all = pos_code[:, :tok_rows] * RUN + pos_code[:, tok_rows:]
        pos_halves = key_pos_all.reshape(total_runs, RUN)
        run_of_half = pos_halves[:, 0] // RUN
        half_of_run = jnp.zeros((total_runs,), jnp.int32).at[run_of_half].set(
            jnp.arange(total_runs, dtype=jnp.int32)
        )

        q_pos = row_map.reshape(runs_here, RUN)
        q_start = (row_map - in_doc).reshape(runs_here, RUN)
        q_run = q_pos[:, 0] // RUN
        first_run = jnp.maximum(q_run - (win_runs - 1), 0)
        win = first_run[:, None] + jnp.arange(win_runs, dtype=jnp.int32)[None, :]
        win_halves = half_of_run[win]
        units = blk_rows // 8
        half_block = win_halves // 2
        piece_of = half_block // nz
        unit0 = (half_block % nz) * units + (win_halves % 2) * (RUN // 8)
        unit_idx = unit0[..., None] + jnp.arange(RUN // 8, dtype=jnp.int32)
        kv_win = None
        for p, piece in enumerate(kv_pieces):
            got = piece.reshape(nz * units, 8, 2 * kv_cols)[unit_idx]
            kv_win = got if kv_win is None else jnp.where((piece_of == p)[..., None, None, None], got, kv_win)
        kv_win = kv_win.reshape(runs_here, win_runs * RUN, 2 * kv_cols)
        k_pos = pos_halves[win_halves].reshape(runs_here, win_runs * RUN)
        k_win = kv_win[..., :kv_cols]
        v_win = kv_win[..., kv_cols:]

        q_runs = queries.reshape(runs_here, RUN, group_size, HEAD_DIM)
        scale_factor = HEAD_DIM ** (-0.5)
        scores = (
            jnp.einsum("rqgd,rkd->rgqk", q_runs, k_win, preferred_element_type=jnp.float32)
            * scale_factor
        )
        allowed = (k_pos[:, None, :] >= q_start[:, :, None]) & (k_pos[:, None, :] <= q_pos[:, :, None])
        allowed = allowed[:, None]
        scores = jnp.where(allowed, scores, NEG_FILL)
        row_top = jnp.max(scores, -1, keepdims=True)
        weights = jnp.where(allowed, jnp.exp(scores - row_top), 0.0)
        row_sum = jnp.sum(weights, -1, keepdims=True)
        mixed = (
            jnp.einsum(
                "rgqk,rkd->rgqd", weights.astype(jnp.bfloat16), v_win,
                preferred_element_type=jnp.float32,
            )
            / row_sum
        ).astype(jnp.bfloat16)
        attended = jnp.transpose(mixed, (0, 2, 1, 3)).reshape(tok_rows, q_cols)

        partial_g = jnp.einsum(
            "tk,jdk->tjd", attended, w_o,
            preferred_element_type=jnp.float32,
        )
        partial_out = from_gathered_order(partial_g, sizes).reshape(tok_rows, width)
        head_share = reduce_scatter_head(partial_out, head_sizes)
        col_width = head_share.shape[1]
        head_idx = lax.axis_index("y") * head_sizes[1] + lax.axis_index("xl")
        own_cols = lax.dynamic_slice_in_dim(tokens, head_idx * col_width, col_width, 1)
        residual_out = (own_cols.astype(jnp.float32) + head_share).astype(jnp.bfloat16)

        is_last = row_map[:, None] == (doc_ends - 1)[None, :]
        label_f = doc_labels.astype(jnp.float32)
        harmful = jnp.sum(label_f)
        harmless = doc_labels.shape[0] - jnp.sum(label_f)
        stream = residual_out.astype(jnp.float32)
        harm_rows = jnp.sum(jnp.where(is_last, label_f[None, :], 0.0), 1)
        safe_rows = jnp.sum(jnp.where(is_last, (1.0 - label_f)[None, :], 0.0), 1)
        sums = jnp.stack(
            [jnp.sum(harm_rows[:, None] * stream, 0), jnp.sum(safe_rows[:, None] * stream, 0)]
        )
        for axis in ("c", "xh", "z"):
            sums = lax.psum(sums, axis)
        refusal_direction = sums[0] / harmful - sums[1] / harmless
        return (residual_out, refusal_direction)

    return local


def solution(mesh):
    n_ctx = mesh.shape["ctx"]
    n_head = mesh.shape["head"]
    nc, nxh = 2, 2
    nz = n_ctx // (nc * nxh)
    ny, nxl = n_head // 2, 2
    fine = Mesh(mesh.devices.reshape(nz, nxh, nc, ny, nxl), ("z", "xh", "c", "y", "xl"))
    placed = (
        P(CTX, None),
        P(),
        P(CTX, HEAD),
        P(CTX, HEAD),
        P(CTX, HEAD),
        P(HEAD, CTX),
        P(CTX),
        P(),
        P(),
    )
    return jax.shard_map(
        make_local((nz, nxh, nc), (ny, nxl)),
        mesh=fine,
        in_specs=placed,
        out_specs=(P(CTX, HEAD), P(HEAD)),
        check_vma=False,
    )
```

```python
import math

import jax
import jax.numpy as jnp
from jax import lax
from jax.sharding import Mesh
from jax.sharding import PartitionSpec as P

HEADS = 32
KV_HEADS = 8
HEAD_DIM = 128
MOST = 2048
RUN = 64

ROPE_BASE = 500000.0
NEG_FILL = -1e30

CTX = ("z", "xh", "c")
HEAD = ("y", "xl")


def doc_layout(row_map, doc_lengths):
    doc_ends = jnp.cumsum(doc_lengths)
    doc_starts = doc_ends - doc_lengths
    doc_index = jnp.sum((row_map[:, None] >= doc_ends[None, :]).astype(jnp.int32), 1)
    member = doc_index[:, None] == jnp.arange(doc_ends.shape[0], dtype=jnp.int32)[None, :]
    in_doc = row_map - jnp.sum(jnp.where(member, doc_starts[None, :], 0), 1)
    return (doc_index, in_doc, doc_ends)


def rotate(values, in_doc):
    head_dim = values.shape[-1]
    half_dim = head_dim // 2
    inv_freq = jnp.exp(
        jnp.arange(half_dim).astype(jnp.float32) * (-2.0 * math.log(ROPE_BASE) / head_dim)
    )
    angles = in_doc.astype(jnp.float32)[:, None] * inv_freq[None, :]
    shape_out = (angles.shape[0],) + (1,) * (values.ndim - 2) + (half_dim,)
    cosine = jnp.cos(angles).reshape(shape_out)
    sine_val = jnp.sin(angles).reshape(shape_out)
    front_half = values[..., :half_dim]
    back_half = values[..., half_dim:]
    return jnp.concatenate(
        [front_half * cosine - back_half * sine_val, back_half * cosine + front_half * sine_val], -1
    )


def rms_norm(tokens, norm_gain):
    wide_tokens = tokens.astype(jnp.float32)
    row_scale = lax.rsqrt(jnp.mean(wide_tokens * wide_tokens, -1, keepdims=True) + 1e-05)
    return (wide_tokens * row_scale * norm_gain).astype(jnp.bfloat16)


def swap_cat(x, axis_name):
    return jnp.concatenate([x, lax.ppermute(x, axis_name, [(0, 1), (1, 0)])], 0)


def gather_z(x):
    return lax.all_gather(x, "z", axis=0, tiled=True)


def gather_pair(x):
    return swap_cat(swap_cat(x, "xh"), "c")


def relative_index():
    return (
        lax.axis_index("c") ^ jnp.arange(2, dtype=jnp.int32),
        lax.axis_index("xh") ^ jnp.arange(2, dtype=jnp.int32),
    )


def to_gathered_order(x, sizes):
    nz, nxh, nc = sizes
    c_idx, xh_idx = relative_index()
    y = jnp.transpose(x.reshape(x.shape[0], nz, nxh, nc, x.shape[-1]), (0, 3, 2, 1, 4))
    y = jnp.take(jnp.take(y, c_idx, axis=1), xh_idx, axis=2)
    return y.reshape(x.shape)


def from_gathered_order(x, sizes):
    nz, nxh, nc = sizes
    c_idx, xh_idx = relative_index()
    y = x.reshape(x.shape[0], nc, nxh, nz, x.shape[-1])
    y = jnp.take(jnp.take(y, c_idx, axis=1), xh_idx, axis=2)
    return jnp.transpose(y, (0, 3, 2, 1, 4)).reshape(x.shape)


def reduce_scatter_head(x, head_sizes):
    ny, nxl = head_sizes
    rows, width = x.shape
    xl = lax.axis_index("xl")
    y = lax.axis_index("y")
    grouped = x.reshape(rows, ny, nxl, width // (ny * nxl))
    kept = jnp.take(grouped, xl, axis=2)
    sent = jnp.take(grouped, (xl + 1) % nxl, axis=2).astype(jnp.bfloat16)
    summed = kept + lax.ppermute(sent, "xl", [(0, 1), (1, 0)]).astype(jnp.float32)
    acc = jnp.take(summed, y, axis=1)
    for shift in range(1, ny):
        piece = jnp.take(summed, (y + shift) % ny, axis=1).astype(jnp.bfloat16)
        acc = acc + lax.ppermute(
            piece, "y", [(i, (i + shift) % ny) for i in range(ny)]
        ).astype(jnp.float32)
    return acc


def make_local(sizes, head_sizes):
    nz, nxh, nc = sizes
    nctx = nz * nxh * nc

    def local(tokens, norm_gain, w_query, w_key, w_value, w_out, row_map, doc_lengths, doc_labels):
        tok_rows, width = tokens.shape
        d_rows = w_query.shape[0]
        q_cols = w_query.shape[1]
        kv_cols = w_key.shape[1]
        group_size = q_cols // kv_cols
        runs_here = tok_rows // RUN
        total_runs = runs_here * nctx
        win_runs = MOST // RUN + 1

        normed = rms_norm(tokens, norm_gain)
        doc_index, in_doc, doc_ends = doc_layout(row_map, doc_lengths)

        qkv_cols = q_cols + 2 * kv_cols
        out_cols = w_out.shape[0]
        w_z = gather_z(jnp.concatenate([w_query, w_key, w_value, w_out.T], axis=1))
        w_o = gather_pair(w_z[:, qkv_cols:]).reshape(nctx, d_rows, out_cols)
        w_proj = w_z[:, :qkv_cols]

        pair = ("xh", "c")
        npair = nxh * nc
        me = lax.axis_index("xh") * nc + lax.axis_index("c")
        quarters = jnp.transpose(
            normed.reshape(tok_rows, nz, nxh, nc, d_rows), (0, 2, 3, 1, 4)
        ).reshape(tok_rows, npair, nz * d_rows)
        perms = [[(i, i ^ flip) for i in range(npair)] for flip in range(1, npair)]
        theirs = [
            lax.ppermute(jnp.take(quarters, me ^ flip, axis=1), pair, perm)
            for flip, perm in zip(range(1, npair), perms)
        ]
        stacked = jnp.concatenate([jnp.take(quarters, me, axis=1)] + theirs, axis=0)
        parts = jnp.dot(stacked, w_proj, preferred_element_type=jnp.float32)
        proj = parts[:tok_rows]
        for k, perm in enumerate(perms):
            proj = proj + lax.ppermute(parts[(k + 1) * tok_rows : (k + 2) * tok_rows], pair, perm)
        queries = proj[:, :q_cols].reshape(tok_rows, group_size, HEAD_DIM)
        key_proj = proj[:, q_cols : q_cols + kv_cols]
        value_proj = proj[:, q_cols + kv_cols :].astype(jnp.bfloat16)
        queries = rotate(queries, in_doc).astype(jnp.bfloat16)
        key_proj = rotate(key_proj, in_doc).astype(jnp.bfloat16)

        assert 2 * tok_rows == 2 * kv_cols
        pos_row = jnp.concatenate([row_map // RUN, row_map % RUN]).astype(jnp.bfloat16)[None, :]
        kv_buf = jnp.concatenate(
            [jnp.concatenate([key_proj, value_proj], axis=1), jnp.pad(pos_row, ((0, 7), (0, 0)))],
            axis=0,
        )
        kv = gather_pair(gather_z(kv_buf)).reshape(nctx, tok_rows + 8, 2 * kv_cols)
        pos_code = kv[:, tok_rows, :].astype(jnp.int32)
        key_pos_all = pos_code[:, :tok_rows] * RUN + pos_code[:, tok_rows:]
        kv_halves = kv[:, :tok_rows].reshape(total_runs, RUN, 2 * kv_cols)
        pos_halves = key_pos_all.reshape(total_runs, RUN)
        run_of_half = pos_halves[:, 0] // RUN
        half_of_run = jnp.zeros((total_runs,), jnp.int32).at[run_of_half].set(
            jnp.arange(total_runs, dtype=jnp.int32)
        )

        q_pos = row_map.reshape(runs_here, RUN)
        q_start = (row_map - in_doc).reshape(runs_here, RUN)
        q_run = q_pos[:, 0] // RUN
        first_run = jnp.maximum(q_run - (win_runs - 1), 0)
        win = first_run[:, None] + jnp.arange(win_runs, dtype=jnp.int32)[None, :]
        win_halves = half_of_run[win]
        kv_win = kv_halves[win_halves].reshape(runs_here, win_runs * RUN, 2 * kv_cols)
        k_pos = pos_halves[win_halves].reshape(runs_here, win_runs * RUN)
        k_win = kv_win[..., :kv_cols]
        v_win = kv_win[..., kv_cols:]

        q_runs = queries.reshape(runs_here, RUN, group_size, HEAD_DIM)
        scale_factor = HEAD_DIM ** (-0.5)
        scores = (
            jnp.einsum("rqgd,rkd->rgqk", q_runs, k_win, preferred_element_type=jnp.float32)
            * scale_factor
        )
        allowed = (k_pos[:, None, :] >= q_start[:, :, None]) & (k_pos[:, None, :] <= q_pos[:, :, None])
        allowed = allowed[:, None]
        scores = jnp.where(allowed, scores, NEG_FILL)
        row_top = jnp.max(scores, -1, keepdims=True)
        weights = jnp.where(allowed, jnp.exp(scores - row_top), 0.0)
        row_sum = jnp.sum(weights, -1, keepdims=True)
        mixed = (
            jnp.einsum(
                "rgqk,rkd->rgqd", weights.astype(jnp.bfloat16), v_win,
                preferred_element_type=jnp.float32,
            )
            / row_sum
        ).astype(jnp.bfloat16)
        attended = jnp.transpose(mixed, (0, 2, 1, 3)).reshape(tok_rows, q_cols)

        partial_g = jnp.einsum(
            "tk,jdk->tjd", attended, w_o,
            preferred_element_type=jnp.float32,
        )
        partial_out = from_gathered_order(partial_g, sizes).reshape(tok_rows, width)
        head_share = reduce_scatter_head(partial_out, head_sizes)
        col_width = head_share.shape[1]
        head_idx = lax.axis_index("y") * head_sizes[1] + lax.axis_index("xl")
        own_cols = lax.dynamic_slice_in_dim(tokens, head_idx * col_width, col_width, 1)
        residual_out = (own_cols.astype(jnp.float32) + head_share).astype(jnp.bfloat16)

        is_last = row_map[:, None] == (doc_ends - 1)[None, :]
        label_f = doc_labels.astype(jnp.float32)
        harmful = jnp.sum(label_f)
        harmless = doc_labels.shape[0] - jnp.sum(label_f)
        stream = residual_out.astype(jnp.float32)
        harm_rows = jnp.sum(jnp.where(is_last, label_f[None, :], 0.0), 1)
        safe_rows = jnp.sum(jnp.where(is_last, (1.0 - label_f)[None, :], 0.0), 1)
        sums = jnp.stack(
            [jnp.sum(harm_rows[:, None] * stream, 0), jnp.sum(safe_rows[:, None] * stream, 0)]
        )
        for axis in ("c", "xh", "z"):
            sums = lax.psum(sums, axis)
        refusal_direction = sums[0] / harmful - sums[1] / harmless
        return (residual_out, refusal_direction)

    return local


def solution(mesh):
    n_ctx = mesh.shape["ctx"]
    n_head = mesh.shape["head"]
    nc, nxh = 2, 2
    nz = n_ctx // (nc * nxh)
    ny, nxl = n_head // 2, 2
    fine = Mesh(mesh.devices.reshape(nz, nxh, nc, ny, nxl), ("z", "xh", "c", "y", "xl"))
    placed = (
        P(CTX, None),
        P(),
        P(CTX, HEAD),
        P(CTX, HEAD),
        P(CTX, HEAD),
        P(HEAD, CTX),
        P(CTX),
        P(),
        P(),
    )
    return jax.shard_map(
        make_local((nz, nxh, nc), (ny, nxl)),
        mesh=fine,
        in_specs=placed,
        out_specs=(P(CTX, HEAD), P(HEAD)),
        check_vma=False,
    )
```

```python
import math

import jax
import jax.numpy as jnp
from jax import lax
from jax.sharding import Mesh
from jax.sharding import PartitionSpec as P

HEADS = 32
KV_HEADS = 8
HEAD_DIM = 128
MOST = 2048
RUN = 64

ROPE_BASE = 500000.0
NEG_FILL = -1e30

CTX = ("z", "xh", "c")
HEAD = ("y", "xl")


def doc_layout(row_map, doc_lengths):
    doc_ends = jnp.cumsum(doc_lengths)
    doc_starts = doc_ends - doc_lengths
    doc_index = jnp.sum((row_map[:, None] >= doc_ends[None, :]).astype(jnp.int32), 1)
    member = doc_index[:, None] == jnp.arange(doc_ends.shape[0], dtype=jnp.int32)[None, :]
    in_doc = row_map - jnp.sum(jnp.where(member, doc_starts[None, :], 0), 1)
    return (doc_index, in_doc, doc_ends)


def rotate(values, in_doc):
    head_dim = values.shape[-1]
    half_dim = head_dim // 2
    inv_freq = jnp.exp(
        jnp.arange(half_dim).astype(jnp.float32) * (-2.0 * math.log(ROPE_BASE) / head_dim)
    )
    angles = in_doc.astype(jnp.float32)[:, None] * inv_freq[None, :]
    shape_out = (angles.shape[0],) + (1,) * (values.ndim - 2) + (half_dim,)
    cosine = jnp.cos(angles).reshape(shape_out)
    sine_val = jnp.sin(angles).reshape(shape_out)
    front_half = values[..., :half_dim]
    back_half = values[..., half_dim:]
    return jnp.concatenate(
        [front_half * cosine - back_half * sine_val, back_half * cosine + front_half * sine_val], -1
    )


def rms_norm(tokens, norm_gain):
    wide_tokens = tokens.astype(jnp.float32)
    row_scale = lax.rsqrt(jnp.mean(wide_tokens * wide_tokens, -1, keepdims=True) + 1e-05)
    return (wide_tokens * row_scale * norm_gain).astype(jnp.bfloat16)


def swap_cat(x, axis_name):
    return jnp.concatenate([x, lax.ppermute(x, axis_name, [(0, 1), (1, 0)])], 0)


def gather_z(x):
    return lax.all_gather(x, "z", axis=0, tiled=True)


def gather_pair(x):
    return swap_cat(swap_cat(x, "xh"), "c")


def ring_gather(x, axis_name, n):
    fwd, bwd = x, x
    by_offset = {0: x}
    for step in range(1, n // 2 + 1):
        fwd = lax.ppermute(fwd, axis_name, [(i, (i + 1) % n) for i in range(n)])
        by_offset[n - step] = fwd
        if len(by_offset) < n:
            bwd = lax.ppermute(bwd, axis_name, [(i, (i - 1) % n) for i in range(n)])
            by_offset[step] = bwd
    rel = jnp.stack([by_offset[k] for k in range(n)])
    here = lax.axis_index(axis_name)
    absolute = jnp.take(rel, (jnp.arange(n, dtype=jnp.int32) - here) % n, axis=0)
    return absolute.reshape((n * x.shape[0],) + x.shape[1:])


def relative_index():
    return (
        lax.axis_index("c") ^ jnp.arange(2, dtype=jnp.int32),
        lax.axis_index("xh") ^ jnp.arange(2, dtype=jnp.int32),
    )


def to_gathered_order(x, sizes):
    nz, nxh, nc = sizes
    c_idx, xh_idx = relative_index()
    y = jnp.transpose(x.reshape(x.shape[0], nz, nxh, nc, x.shape[-1]), (0, 3, 2, 1, 4))
    y = jnp.take(jnp.take(y, c_idx, axis=1), xh_idx, axis=2)
    return y.reshape(x.shape)


def from_gathered_order(x, sizes):
    nz, nxh, nc = sizes
    c_idx, xh_idx = relative_index()
    y = x.reshape(x.shape[0], nc, nxh, nz, x.shape[-1])
    y = jnp.take(jnp.take(y, c_idx, axis=1), xh_idx, axis=2)
    return jnp.transpose(y, (0, 3, 2, 1, 4)).reshape(x.shape)


def reduce_scatter_head(x, head_sizes):
    ny, nxl = head_sizes
    rows, width = x.shape
    xl = lax.axis_index("xl")
    y = lax.axis_index("y")
    grouped = x.reshape(rows, ny, nxl, width // (ny * nxl))
    kept = jnp.take(grouped, xl, axis=2)
    sent = jnp.take(grouped, (xl + 1) % nxl, axis=2).astype(jnp.bfloat16)
    summed = kept + lax.ppermute(sent, "xl", [(0, 1), (1, 0)]).astype(jnp.float32)
    acc = jnp.take(summed, y, axis=1)
    for shift in range(1, ny):
        piece = jnp.take(summed, (y + shift) % ny, axis=1).astype(jnp.bfloat16)
        acc = acc + lax.ppermute(
            piece, "y", [(i, (i + shift) % ny) for i in range(ny)]
        ).astype(jnp.float32)
    return acc


def make_local(sizes, head_sizes):
    nz, nxh, nc = sizes
    nctx = nz * nxh * nc

    def local(tokens, norm_gain, w_query, w_key, w_value, w_out, row_map, doc_lengths, doc_labels):
        tok_rows, width = tokens.shape
        d_rows = w_query.shape[0]
        q_cols = w_query.shape[1]
        kv_cols = w_key.shape[1]
        group_size = q_cols // kv_cols
        runs_here = tok_rows // RUN
        total_runs = runs_here * nctx
        win_runs = MOST // RUN + 1

        normed = rms_norm(tokens, norm_gain)
        doc_index, in_doc, doc_ends = doc_layout(row_map, doc_lengths)

        out_cols = w_out.shape[0]
        w_z = gather_z(jnp.concatenate([w_key, w_value, w_out.T], axis=1))
        w_kv = w_z[:, : 2 * kv_cols]
        w_o = gather_pair(w_z[:, 2 * kv_cols :]).reshape(nctx, d_rows, out_cols)
        w_q = ring_gather(w_query, "z", nz)

        pair = ("xh", "c")
        npair = nxh * nc
        me = lax.axis_index("xh") * nc + lax.axis_index("c")
        quarters = jnp.transpose(
            normed.reshape(tok_rows, nz, nxh, nc, d_rows), (0, 2, 3, 1, 4)
        ).reshape(tok_rows, npair, nz * d_rows)
        perms = [[(i, i ^ flip) for i in range(npair)] for flip in range(1, npair)]
        theirs = [
            lax.ppermute(jnp.take(quarters, me ^ flip, axis=1), pair, perm)
            for flip, perm in zip(range(1, npair), perms)
        ]
        stacked = jnp.concatenate([jnp.take(quarters, me, axis=1)] + theirs, axis=0)

        def exchange(weights):
            parts = jnp.dot(stacked, weights, preferred_element_type=jnp.float32)
            total = parts[:tok_rows]
            for k, perm in enumerate(perms):
                total = total + lax.ppermute(
                    parts[(k + 1) * tok_rows : (k + 2) * tok_rows], pair, perm
                )
            return total

        proj_kv = exchange(w_kv)
        proj_q = exchange(w_q)
        queries = proj_q.reshape(tok_rows, group_size, HEAD_DIM)
        key_proj = proj_kv[:, :kv_cols]
        value_proj = proj_kv[:, kv_cols:].astype(jnp.bfloat16)
        queries = rotate(queries, in_doc).astype(jnp.bfloat16)
        key_proj = rotate(key_proj, in_doc).astype(jnp.bfloat16)

        assert 2 * tok_rows == 2 * kv_cols
        pos_row = jnp.concatenate([row_map // RUN, row_map % RUN]).astype(jnp.bfloat16)[None, :]
        kv_buf = jnp.concatenate(
            [jnp.concatenate([key_proj, value_proj], axis=1), jnp.pad(pos_row, ((0, 7), (0, 0)))],
            axis=0,
        )
        kv = gather_pair(gather_z(kv_buf)).reshape(nctx, tok_rows + 8, 2 * kv_cols)
        pos_code = kv[:, tok_rows, :].astype(jnp.int32)
        key_pos_all = pos_code[:, :tok_rows] * RUN + pos_code[:, tok_rows:]
        kv_halves = kv[:, :tok_rows].reshape(total_runs, RUN, 2 * kv_cols)
        pos_halves = key_pos_all.reshape(total_runs, RUN)
        run_of_half = pos_halves[:, 0] // RUN
        half_of_run = jnp.zeros((total_runs,), jnp.int32).at[run_of_half].set(
            jnp.arange(total_runs, dtype=jnp.int32)
        )

        q_pos = row_map.reshape(runs_here, RUN)
        q_start = (row_map - in_doc).reshape(runs_here, RUN)
        q_run = q_pos[:, 0] // RUN
        first_run = jnp.maximum(q_run - (win_runs - 1), 0)
        win = first_run[:, None] + jnp.arange(win_runs, dtype=jnp.int32)[None, :]
        win_halves = half_of_run[win]
        kv_win = kv_halves[win_halves].reshape(runs_here, win_runs * RUN, 2 * kv_cols)
        k_pos = pos_halves[win_halves].reshape(runs_here, win_runs * RUN)
        k_win = kv_win[..., :kv_cols]
        v_win = kv_win[..., kv_cols:]

        q_runs = queries.reshape(runs_here, RUN, group_size, HEAD_DIM)
        scale_factor = HEAD_DIM ** (-0.5)
        scores = (
            jnp.einsum("rqgd,rkd->rgqk", q_runs, k_win, preferred_element_type=jnp.float32)
            * scale_factor
        )
        allowed = (k_pos[:, None, :] >= q_start[:, :, None]) & (k_pos[:, None, :] <= q_pos[:, :, None])
        allowed = allowed[:, None]
        scores = jnp.where(allowed, scores, NEG_FILL)
        row_top = jnp.max(scores, -1, keepdims=True)
        weights = jnp.where(allowed, jnp.exp(scores - row_top), 0.0)
        row_sum = jnp.sum(weights, -1, keepdims=True)
        mixed = (
            jnp.einsum(
                "rgqk,rkd->rgqd", weights.astype(jnp.bfloat16), v_win,
                preferred_element_type=jnp.float32,
            )
            / row_sum
        ).astype(jnp.bfloat16)
        attended = jnp.transpose(mixed, (0, 2, 1, 3)).reshape(tok_rows, q_cols)

        partial_g = jnp.einsum(
            "tk,jdk->tjd", attended, w_o,
            preferred_element_type=jnp.float32,
        )
        partial_out = from_gathered_order(partial_g, sizes).reshape(tok_rows, width)
        head_share = reduce_scatter_head(partial_out, head_sizes)
        col_width = head_share.shape[1]
        head_idx = lax.axis_index("y") * head_sizes[1] + lax.axis_index("xl")
        own_cols = lax.dynamic_slice_in_dim(tokens, head_idx * col_width, col_width, 1)
        residual_out = (own_cols.astype(jnp.float32) + head_share).astype(jnp.bfloat16)

        is_last = row_map[:, None] == (doc_ends - 1)[None, :]
        label_f = doc_labels.astype(jnp.float32)
        harmful = jnp.sum(label_f)
        harmless = doc_labels.shape[0] - jnp.sum(label_f)
        stream = residual_out.astype(jnp.float32)
        harm_rows = jnp.sum(jnp.where(is_last, label_f[None, :], 0.0), 1)
        safe_rows = jnp.sum(jnp.where(is_last, (1.0 - label_f)[None, :], 0.0), 1)
        sums = jnp.stack(
            [jnp.sum(harm_rows[:, None] * stream, 0), jnp.sum(safe_rows[:, None] * stream, 0)]
        )
        for axis in ("c", "xh", "z"):
            sums = lax.psum(sums, axis)
        refusal_direction = sums[0] / harmful - sums[1] / harmless
        return (residual_out, refusal_direction)

    return local


def solution(mesh):
    n_ctx = mesh.shape["ctx"]
    n_head = mesh.shape["head"]
    nc, nxh = 2, 2
    nz = n_ctx // (nc * nxh)
    ny, nxl = n_head // 2, 2
    fine = Mesh(mesh.devices.reshape(nz, nxh, nc, ny, nxl), ("z", "xh", "c", "y", "xl"))
    placed = (
        P(CTX, None),
        P(),
        P(CTX, HEAD),
        P(CTX, HEAD),
        P(CTX, HEAD),
        P(HEAD, CTX),
        P(CTX),
        P(),
        P(),
    )
    return jax.shard_map(
        make_local((nz, nxh, nc), (ny, nxl)),
        mesh=fine,
        in_specs=placed,
        out_specs=(P(CTX, HEAD), P(HEAD)),
        check_vma=False,
    )
```

```python
import math

import jax
import jax.numpy as jnp
from jax import lax
from jax.sharding import Mesh
from jax.sharding import PartitionSpec as P

HEADS = 32
KV_HEADS = 8
HEAD_DIM = 128
MOST = 2048
RUN = 64

ROPE_BASE = 500000.0
NEG_FILL = -1e30

CTX = ("z", "xh", "c")
HEAD = ("y", "xl")


def doc_layout(row_map, doc_lengths):
    doc_ends = jnp.cumsum(doc_lengths)
    doc_starts = doc_ends - doc_lengths
    doc_index = jnp.sum((row_map[:, None] >= doc_ends[None, :]).astype(jnp.int32), 1)
    member = doc_index[:, None] == jnp.arange(doc_ends.shape[0], dtype=jnp.int32)[None, :]
    in_doc = row_map - jnp.sum(jnp.where(member, doc_starts[None, :], 0), 1)
    return (doc_index, in_doc, doc_ends)


def rotate(values, in_doc):
    head_dim = values.shape[-1]
    half_dim = head_dim // 2
    inv_freq = jnp.exp(
        jnp.arange(half_dim).astype(jnp.float32) * (-2.0 * math.log(ROPE_BASE) / head_dim)
    )
    angles = in_doc.astype(jnp.float32)[:, None] * inv_freq[None, :]
    shape_out = (angles.shape[0],) + (1,) * (values.ndim - 2) + (half_dim,)
    cosine = jnp.cos(angles).reshape(shape_out)
    sine_val = jnp.sin(angles).reshape(shape_out)
    front_half = values[..., :half_dim]
    back_half = values[..., half_dim:]
    return jnp.concatenate(
        [front_half * cosine - back_half * sine_val, back_half * cosine + front_half * sine_val], -1
    )


def rms_norm(tokens, norm_gain):
    wide_tokens = tokens.astype(jnp.float32)
    row_scale = lax.rsqrt(jnp.mean(wide_tokens * wide_tokens, -1, keepdims=True) + 1e-05)
    return (wide_tokens * row_scale * norm_gain).astype(jnp.bfloat16)


def swap_cat(x, axis_name):
    return jnp.concatenate([x, lax.ppermute(x, axis_name, [(0, 1), (1, 0)])], 0)


def gather_z(x):
    return lax.all_gather(x, "z", axis=0, tiled=True)


def gather_pair(x):
    return swap_cat(swap_cat(x, "xh"), "c")


def relative_index():
    return (
        lax.axis_index("c") ^ jnp.arange(2, dtype=jnp.int32),
        lax.axis_index("xh") ^ jnp.arange(2, dtype=jnp.int32),
    )


def to_gathered_order(x, sizes):
    nz, nxh, nc = sizes
    c_idx, xh_idx = relative_index()
    y = jnp.transpose(x.reshape(x.shape[0], nz, nxh, nc, x.shape[-1]), (0, 3, 2, 1, 4))
    y = jnp.take(jnp.take(y, c_idx, axis=1), xh_idx, axis=2)
    return y.reshape(x.shape)


def from_gathered_order(x, sizes):
    nz, nxh, nc = sizes
    c_idx, xh_idx = relative_index()
    y = x.reshape(x.shape[0], nc, nxh, nz, x.shape[-1])
    y = jnp.take(jnp.take(y, c_idx, axis=1), xh_idx, axis=2)
    return jnp.transpose(y, (0, 3, 2, 1, 4)).reshape(x.shape)


def reduce_scatter_head(x, head_sizes):
    ny, nxl = head_sizes
    rows, width = x.shape
    xl = lax.axis_index("xl")
    y = lax.axis_index("y")
    grouped = x.reshape(rows, ny, nxl, width // (ny * nxl))
    kept = jnp.take(grouped, xl, axis=2)
    sent = jnp.take(grouped, (xl + 1) % nxl, axis=2).astype(jnp.bfloat16)
    summed = kept + lax.ppermute(sent, "xl", [(0, 1), (1, 0)]).astype(jnp.float32)
    acc = jnp.take(summed, y, axis=1)
    for shift in range(1, ny):
        piece = jnp.take(summed, (y + shift) % ny, axis=1).astype(jnp.bfloat16)
        acc = acc + lax.ppermute(
            piece, "y", [(i, (i + shift) % ny) for i in range(ny)]
        ).astype(jnp.float32)
    return acc


def make_local(sizes, head_sizes):
    nz, nxh, nc = sizes
    nctx = nz * nxh * nc

    def local(tokens, norm_gain, w_query, w_key, w_value, w_out, row_map, doc_lengths, doc_labels):
        tok_rows, width = tokens.shape
        d_rows = w_query.shape[0]
        q_cols = w_query.shape[1]
        kv_cols = w_key.shape[1]
        group_size = q_cols // kv_cols
        runs_here = tok_rows // RUN
        total_runs = runs_here * nctx
        win_runs = MOST // RUN + 1

        normed = rms_norm(tokens, norm_gain)
        doc_index, in_doc, doc_ends = doc_layout(row_map, doc_lengths)

        qkv_cols = q_cols + 2 * kv_cols
        out_cols = w_out.shape[0]
        w_z = gather_z(jnp.concatenate([w_query, w_key, w_value, w_out.T], axis=1))
        w_o = gather_pair(w_z[:, qkv_cols:]).reshape(nctx, d_rows, out_cols)
        w_proj = w_z[:, :qkv_cols]

        pair = ("xh", "c")
        npair = nxh * nc
        me = lax.axis_index("xh") * nc + lax.axis_index("c")
        quarters = jnp.transpose(
            normed.reshape(tok_rows, nz, nxh, nc, d_rows), (0, 2, 3, 1, 4)
        ).reshape(tok_rows, npair, nz * d_rows)
        perms = [[(i, i ^ flip) for i in range(npair)] for flip in range(1, npair)]
        theirs = [
            lax.ppermute(jnp.take(quarters, me ^ flip, axis=1), pair, perm)
            for flip, perm in zip(range(1, npair), perms)
        ]
        stacked = jnp.concatenate([jnp.take(quarters, me, axis=1)] + theirs, axis=0)
        parts = jnp.dot(stacked, w_proj, preferred_element_type=jnp.float32)
        rows = tok_rows
        on_chip = lax.ppermute(
            jnp.concatenate([parts[rows : 2 * rows], parts[3 * rows : 4 * rows]]), pair, perms[0]
        )
        across = lax.ppermute(parts[2 * rows : 3 * rows] + on_chip[rows:], pair, perms[1])
        proj = parts[:rows] + on_chip[:rows] + across
        queries = proj[:, :q_cols].reshape(tok_rows, group_size, HEAD_DIM)
        key_proj = proj[:, q_cols : q_cols + kv_cols]
        value_proj = proj[:, q_cols + kv_cols :].astype(jnp.bfloat16)
        queries = rotate(queries, in_doc).astype(jnp.bfloat16)
        key_proj = rotate(key_proj, in_doc).astype(jnp.bfloat16)

        assert 2 * tok_rows == 2 * kv_cols
        pos_row = jnp.concatenate([row_map // RUN, row_map % RUN]).astype(jnp.bfloat16)[None, :]
        kv_buf = jnp.concatenate(
            [jnp.concatenate([key_proj, value_proj], axis=1), jnp.pad(pos_row, ((0, 7), (0, 0)))],
            axis=0,
        )
        kv = gather_pair(gather_z(kv_buf)).reshape(nctx, tok_rows + 8, 2 * kv_cols)
        pos_code = kv[:, tok_rows, :].astype(jnp.int32)
        key_pos_all = pos_code[:, :tok_rows] * RUN + pos_code[:, tok_rows:]
        kv_halves = kv[:, :tok_rows].reshape(total_runs, RUN, 2 * kv_cols)
        pos_halves = key_pos_all.reshape(total_runs, RUN)
        run_of_half = pos_halves[:, 0] // RUN
        half_of_run = jnp.zeros((total_runs,), jnp.int32).at[run_of_half].set(
            jnp.arange(total_runs, dtype=jnp.int32)
        )

        q_pos = row_map.reshape(runs_here, RUN)
        q_start = (row_map - in_doc).reshape(runs_here, RUN)
        q_run = q_pos[:, 0] // RUN
        first_run = jnp.maximum(q_run - (win_runs - 1), 0)
        win = first_run[:, None] + jnp.arange(win_runs, dtype=jnp.int32)[None, :]
        win_halves = half_of_run[win]
        kv_win = kv_halves[win_halves].reshape(runs_here, win_runs * RUN, 2 * kv_cols)
        k_pos = pos_halves[win_halves].reshape(runs_here, win_runs * RUN)
        k_win = kv_win[..., :kv_cols]
        v_win = kv_win[..., kv_cols:]

        q_runs = queries.reshape(runs_here, RUN, group_size, HEAD_DIM)
        scale_factor = HEAD_DIM ** (-0.5)
        scores = (
            jnp.einsum("rqgd,rkd->rgqk", q_runs, k_win, preferred_element_type=jnp.float32)
            * scale_factor
        )
        allowed = (k_pos[:, None, :] >= q_start[:, :, None]) & (k_pos[:, None, :] <= q_pos[:, :, None])
        allowed = allowed[:, None]
        scores = jnp.where(allowed, scores, NEG_FILL)
        row_top = jnp.max(scores, -1, keepdims=True)
        weights = jnp.where(allowed, jnp.exp(scores - row_top), 0.0)
        row_sum = jnp.sum(weights, -1, keepdims=True)
        mixed = (
            jnp.einsum(
                "rgqk,rkd->rgqd", weights.astype(jnp.bfloat16), v_win,
                preferred_element_type=jnp.float32,
            )
            / row_sum
        ).astype(jnp.bfloat16)
        attended = jnp.transpose(mixed, (0, 2, 1, 3)).reshape(tok_rows, q_cols)

        partial_g = jnp.einsum(
            "tk,jdk->tjd", attended, w_o,
            preferred_element_type=jnp.float32,
        )
        partial_out = from_gathered_order(partial_g, sizes).reshape(tok_rows, width)
        head_share = reduce_scatter_head(partial_out, head_sizes)
        col_width = head_share.shape[1]
        head_idx = lax.axis_index("y") * head_sizes[1] + lax.axis_index("xl")
        own_cols = lax.dynamic_slice_in_dim(tokens, head_idx * col_width, col_width, 1)
        residual_out = (own_cols.astype(jnp.float32) + head_share).astype(jnp.bfloat16)

        is_last = row_map[:, None] == (doc_ends - 1)[None, :]
        label_f = doc_labels.astype(jnp.float32)
        harmful = jnp.sum(label_f)
        harmless = doc_labels.shape[0] - jnp.sum(label_f)
        stream = residual_out.astype(jnp.float32)
        harm_rows = jnp.sum(jnp.where(is_last, label_f[None, :], 0.0), 1)
        safe_rows = jnp.sum(jnp.where(is_last, (1.0 - label_f)[None, :], 0.0), 1)
        sums = jnp.stack(
            [jnp.sum(harm_rows[:, None] * stream, 0), jnp.sum(safe_rows[:, None] * stream, 0)]
        )
        for axis in ("c", "xh", "z"):
            sums = lax.psum(sums, axis)
        refusal_direction = sums[0] / harmful - sums[1] / harmless
        return (residual_out, refusal_direction)

    return local


def solution(mesh):
    n_ctx = mesh.shape["ctx"]
    n_head = mesh.shape["head"]
    nc, nxh = 2, 2
    nz = n_ctx // (nc * nxh)
    ny, nxl = n_head // 2, 2
    fine = Mesh(mesh.devices.reshape(nz, nxh, nc, ny, nxl), ("z", "xh", "c", "y", "xl"))
    placed = (
        P(CTX, None),
        P(),
        P(CTX, HEAD),
        P(CTX, HEAD),
        P(CTX, HEAD),
        P(HEAD, CTX),
        P(CTX),
        P(),
        P(),
    )
    return jax.shard_map(
        make_local((nz, nxh, nc), (ny, nxl)),
        mesh=fine,
        in_specs=placed,
        out_specs=(P(CTX, HEAD), P(HEAD)),
        check_vma=False,
    )
```

```python
import math

import jax
import jax.numpy as jnp
from jax import lax
from jax.sharding import Mesh
from jax.sharding import PartitionSpec as P

HEADS = 32
KV_HEADS = 8
HEAD_DIM = 128
MOST = 2048
RUN = 64

ROPE_BASE = 500000.0
NEG_FILL = -1e30

CTX = ("z", "xh", "c")
HEAD = ("y", "xl")


def doc_layout(row_map, doc_lengths):
    doc_ends = jnp.cumsum(doc_lengths)
    doc_starts = doc_ends - doc_lengths
    doc_index = jnp.sum((row_map[:, None] >= doc_ends[None, :]).astype(jnp.int32), 1)
    member = doc_index[:, None] == jnp.arange(doc_ends.shape[0], dtype=jnp.int32)[None, :]
    in_doc = row_map - jnp.sum(jnp.where(member, doc_starts[None, :], 0), 1)
    return (doc_index, in_doc, doc_ends)


def rotate(values, in_doc):
    head_dim = values.shape[-1]
    half_dim = head_dim // 2
    inv_freq = jnp.exp(
        jnp.arange(half_dim).astype(jnp.float32) * (-2.0 * math.log(ROPE_BASE) / head_dim)
    )
    angles = in_doc.astype(jnp.float32)[:, None] * inv_freq[None, :]
    shape_out = (angles.shape[0],) + (1,) * (values.ndim - 2) + (half_dim,)
    cosine = jnp.cos(angles).reshape(shape_out)
    sine_val = jnp.sin(angles).reshape(shape_out)
    front_half = values[..., :half_dim]
    back_half = values[..., half_dim:]
    return jnp.concatenate(
        [front_half * cosine - back_half * sine_val, back_half * cosine + front_half * sine_val], -1
    )


def rms_norm(tokens, norm_gain):
    wide_tokens = tokens.astype(jnp.float32)
    row_scale = lax.rsqrt(jnp.mean(wide_tokens * wide_tokens, -1, keepdims=True) + 1e-05)
    return (wide_tokens * row_scale * norm_gain).astype(jnp.bfloat16)


def swap_cat(x, axis_name):
    return jnp.concatenate([x, lax.ppermute(x, axis_name, [(0, 1), (1, 0)])], 0)


def gather_z(x):
    return lax.all_gather(x, "z", axis=0, tiled=True)


def gather_pair(x):
    return swap_cat(swap_cat(x, "xh"), "c")


def relative_index():
    return (
        lax.axis_index("c") ^ jnp.arange(2, dtype=jnp.int32),
        lax.axis_index("xh") ^ jnp.arange(2, dtype=jnp.int32),
    )


def to_gathered_order(x, sizes):
    nz, nxh, nc = sizes
    c_idx, xh_idx = relative_index()
    y = jnp.transpose(x.reshape(x.shape[0], nz, nxh, nc, x.shape[-1]), (0, 3, 2, 1, 4))
    y = jnp.take(jnp.take(y, c_idx, axis=1), xh_idx, axis=2)
    return y.reshape(x.shape)


def from_gathered_order(x, sizes):
    nz, nxh, nc = sizes
    c_idx, xh_idx = relative_index()
    y = x.reshape(x.shape[0], nc, nxh, nz, x.shape[-1])
    y = jnp.take(jnp.take(y, c_idx, axis=1), xh_idx, axis=2)
    return jnp.transpose(y, (0, 3, 2, 1, 4)).reshape(x.shape)


def reduce_scatter_head(x, head_sizes):
    ny, nxl = head_sizes
    rows, width = x.shape
    xl = lax.axis_index("xl")
    y = lax.axis_index("y")
    grouped = x.reshape(rows, ny, nxl, width // (ny * nxl))
    kept = jnp.take(grouped, xl, axis=2)
    sent = jnp.take(grouped, (xl + 1) % nxl, axis=2).astype(jnp.bfloat16)
    summed = kept + lax.ppermute(sent, "xl", [(0, 1), (1, 0)]).astype(jnp.float32)
    acc = jnp.take(summed, y, axis=1)
    for shift in range(1, ny):
        piece = jnp.take(summed, (y + shift) % ny, axis=1).astype(jnp.bfloat16)
        acc = acc + lax.ppermute(
            piece, "y", [(i, (i + shift) % ny) for i in range(ny)]
        ).astype(jnp.float32)
    return acc


def make_local(sizes, head_sizes):
    nz, nxh, nc = sizes
    nctx = nz * nxh * nc

    def local(tokens, norm_gain, w_query, w_key, w_value, w_out, row_map, doc_lengths, doc_labels):
        tok_rows, width = tokens.shape
        d_rows = w_query.shape[0]
        q_cols = w_query.shape[1]
        kv_cols = w_key.shape[1]
        group_size = q_cols // kv_cols
        runs_here = tok_rows // RUN
        total_runs = runs_here * nctx
        win_runs = MOST // RUN + 1

        normed = rms_norm(tokens, norm_gain)
        doc_index, in_doc, doc_ends = doc_layout(row_map, doc_lengths)

        qkv_cols = q_cols + 2 * kv_cols
        out_cols = w_out.shape[0]
        w_z = gather_z(jnp.concatenate([w_query, w_key, w_value, w_out.T], axis=1))
        w_o = gather_pair(w_z[:, qkv_cols:]).reshape(nctx, d_rows, out_cols)
        w_proj = w_z[:, :qkv_cols]

        pair = ("xh", "c")
        npair = nxh * nc
        me = lax.axis_index("xh") * nc + lax.axis_index("c")
        quarters = jnp.transpose(
            normed.reshape(tok_rows, nz, nxh, nc, d_rows), (0, 2, 3, 1, 4)
        ).reshape(tok_rows, npair, nz * d_rows)
        perms = [[(i, i ^ flip) for i in range(npair)] for flip in range(1, npair)]
        theirs = [
            lax.ppermute(jnp.take(quarters, me ^ flip, axis=1), pair, perm)
            for flip, perm in zip(range(1, npair), perms)
        ]
        stacked = jnp.concatenate([jnp.take(quarters, me, axis=1)] + theirs, axis=0)
        parts = jnp.dot(stacked, w_proj, preferred_element_type=jnp.float32)
        rows = tok_rows
        on_chip = lax.ppermute(
            jnp.concatenate([parts[rows : 2 * rows], parts[3 * rows : 4 * rows]]), pair, perms[0]
        )
        across = lax.ppermute(parts[2 * rows : 3 * rows] + on_chip[rows:], pair, perms[1])
        proj = parts[:rows] + on_chip[:rows] + across
        queries = proj[:, :q_cols].reshape(tok_rows, group_size, HEAD_DIM)
        key_proj = proj[:, q_cols : q_cols + kv_cols]
        value_proj = proj[:, q_cols + kv_cols :].astype(jnp.bfloat16)
        queries = rotate(queries, in_doc).astype(jnp.bfloat16)
        key_proj = rotate(key_proj, in_doc).astype(jnp.bfloat16)

        assert 2 * tok_rows == 2 * kv_cols
        pos_row = jnp.concatenate([row_map // RUN, row_map % RUN]).astype(jnp.bfloat16)[None, :]
        kv_buf = jnp.concatenate(
            [jnp.concatenate([key_proj, value_proj], axis=1), jnp.pad(pos_row, ((0, 7), (0, 0)))],
            axis=0,
        )
        kv = gather_pair(gather_z(kv_buf)).reshape(nctx, tok_rows + 8, 2 * kv_cols)
        pos_code = kv[:, tok_rows, :].astype(jnp.int32)
        key_pos_all = pos_code[:, :tok_rows] * RUN + pos_code[:, tok_rows:]
        kv_rows = kv.reshape(nctx * (tok_rows + 8), 2 * kv_cols)
        pos_halves = key_pos_all.reshape(total_runs, RUN)
        run_of_half = pos_halves[:, 0] // RUN
        half_of_run = jnp.zeros((total_runs,), jnp.int32).at[run_of_half].set(
            jnp.arange(total_runs, dtype=jnp.int32)
        )

        q_pos = row_map.reshape(runs_here, RUN)
        q_start = (row_map - in_doc).reshape(runs_here, RUN)
        q_run = q_pos[:, 0] // RUN
        first_run = jnp.maximum(q_run - (win_runs - 1), 0)
        win = first_run[:, None] + jnp.arange(win_runs, dtype=jnp.int32)[None, :]
        win_halves = half_of_run[win]
        win_first = (win_halves // 2) * (tok_rows + 8) + (win_halves % 2) * RUN
        win_rows = win_first[..., None] + jnp.arange(RUN, dtype=jnp.int32)
        kv_win = kv_rows[win_rows].reshape(runs_here, win_runs * RUN, 2 * kv_cols)
        k_pos = pos_halves[win_halves].reshape(runs_here, win_runs * RUN)
        k_win = kv_win[..., :kv_cols]
        v_win = kv_win[..., kv_cols:]

        q_runs = queries.reshape(runs_here, RUN, group_size, HEAD_DIM)
        scale_factor = HEAD_DIM ** (-0.5)
        scores = (
            jnp.einsum("rqgd,rkd->rgqk", q_runs, k_win, preferred_element_type=jnp.float32)
            * scale_factor
        )
        allowed = (k_pos[:, None, :] >= q_start[:, :, None]) & (k_pos[:, None, :] <= q_pos[:, :, None])
        allowed = allowed[:, None]
        scores = jnp.where(allowed, scores, NEG_FILL)
        row_top = jnp.max(scores, -1, keepdims=True)
        weights = jnp.where(allowed, jnp.exp(scores - row_top), 0.0)
        row_sum = jnp.sum(weights, -1, keepdims=True)
        mixed = (
            jnp.einsum(
                "rgqk,rkd->rgqd", weights.astype(jnp.bfloat16), v_win,
                preferred_element_type=jnp.float32,
            )
            / row_sum
        ).astype(jnp.bfloat16)
        attended = jnp.transpose(mixed, (0, 2, 1, 3)).reshape(tok_rows, q_cols)

        partial_g = jnp.einsum(
            "tk,jdk->tjd", attended, w_o,
            preferred_element_type=jnp.float32,
        )
        partial_out = from_gathered_order(partial_g, sizes).reshape(tok_rows, width)
        head_share = reduce_scatter_head(partial_out, head_sizes)
        col_width = head_share.shape[1]
        head_idx = lax.axis_index("y") * head_sizes[1] + lax.axis_index("xl")
        own_cols = lax.dynamic_slice_in_dim(tokens, head_idx * col_width, col_width, 1)
        residual_out = (own_cols.astype(jnp.float32) + head_share).astype(jnp.bfloat16)

        is_last = row_map[:, None] == (doc_ends - 1)[None, :]
        label_f = doc_labels.astype(jnp.float32)
        harmful = jnp.sum(label_f)
        harmless = doc_labels.shape[0] - jnp.sum(label_f)
        stream = residual_out.astype(jnp.float32)
        harm_rows = jnp.sum(jnp.where(is_last, label_f[None, :], 0.0), 1)
        safe_rows = jnp.sum(jnp.where(is_last, (1.0 - label_f)[None, :], 0.0), 1)
        sums = jnp.stack(
            [jnp.sum(harm_rows[:, None] * stream, 0), jnp.sum(safe_rows[:, None] * stream, 0)]
        )
        for axis in ("c", "xh", "z"):
            sums = lax.psum(sums, axis)
        refusal_direction = sums[0] / harmful - sums[1] / harmless
        return (residual_out, refusal_direction)

    return local


def solution(mesh):
    n_ctx = mesh.shape["ctx"]
    n_head = mesh.shape["head"]
    nc, nxh = 2, 2
    nz = n_ctx // (nc * nxh)
    ny, nxl = n_head // 2, 2
    fine = Mesh(mesh.devices.reshape(nz, nxh, nc, ny, nxl), ("z", "xh", "c", "y", "xl"))
    placed = (
        P(CTX, None),
        P(),
        P(CTX, HEAD),
        P(CTX, HEAD),
        P(CTX, HEAD),
        P(HEAD, CTX),
        P(CTX),
        P(),
        P(),
    )
    return jax.shard_map(
        make_local((nz, nxh, nc), (ny, nxl)),
        mesh=fine,
        in_specs=placed,
        out_specs=(P(CTX, HEAD), P(HEAD)),
        check_vma=False,
    )
```

```python
import math

import jax
import jax.numpy as jnp
from jax import lax
from jax.sharding import Mesh
from jax.sharding import PartitionSpec as P

HEADS = 32
KV_HEADS = 8
HEAD_DIM = 128
MOST = 2048
RUN = 64

ROPE_BASE = 500000.0
NEG_FILL = -1e30

CTX = ("z", "xh", "c")
HEAD = ("y", "xl")


def doc_layout(row_map, doc_lengths):
    doc_ends = jnp.cumsum(doc_lengths)
    doc_starts = doc_ends - doc_lengths
    doc_index = jnp.sum((row_map[:, None] >= doc_ends[None, :]).astype(jnp.int32), 1)
    member = doc_index[:, None] == jnp.arange(doc_ends.shape[0], dtype=jnp.int32)[None, :]
    in_doc = row_map - jnp.sum(jnp.where(member, doc_starts[None, :], 0), 1)
    return (doc_index, in_doc, doc_ends)


def rotate(values, in_doc):
    head_dim = values.shape[-1]
    half_dim = head_dim // 2
    inv_freq = jnp.exp(
        jnp.arange(half_dim).astype(jnp.float32) * (-2.0 * math.log(ROPE_BASE) / head_dim)
    )
    angles = in_doc.astype(jnp.float32)[:, None] * inv_freq[None, :]
    shape_out = (angles.shape[0],) + (1,) * (values.ndim - 2) + (half_dim,)
    cosine = jnp.cos(angles).reshape(shape_out)
    sine_val = jnp.sin(angles).reshape(shape_out)
    front_half = values[..., :half_dim]
    back_half = values[..., half_dim:]
    return jnp.concatenate(
        [front_half * cosine - back_half * sine_val, back_half * cosine + front_half * sine_val], -1
    )


def rms_norm(tokens, norm_gain):
    wide_tokens = tokens.astype(jnp.float32)
    row_scale = lax.rsqrt(jnp.mean(wide_tokens * wide_tokens, -1, keepdims=True) + 1e-05)
    return (wide_tokens * row_scale * norm_gain).astype(jnp.bfloat16)


def swap_cat(x, axis_name):
    return jnp.concatenate([x, lax.ppermute(x, axis_name, [(0, 1), (1, 0)])], 0)


def gather_z(x):
    return lax.all_gather(x, "z", axis=0, tiled=True)


def gather_pair(x):
    return swap_cat(swap_cat(x, "xh"), "c")


def relative_index():
    return (
        lax.axis_index("c") ^ jnp.arange(2, dtype=jnp.int32),
        lax.axis_index("xh") ^ jnp.arange(2, dtype=jnp.int32),
    )


def to_gathered_order(x, sizes):
    nz, nxh, nc = sizes
    c_idx, xh_idx = relative_index()
    y = jnp.transpose(x.reshape(x.shape[0], nz, nxh, nc, x.shape[-1]), (0, 3, 2, 1, 4))
    y = jnp.take(jnp.take(y, c_idx, axis=1), xh_idx, axis=2)
    return y.reshape(x.shape)


def from_gathered_order(x, sizes):
    nz, nxh, nc = sizes
    c_idx, xh_idx = relative_index()
    y = x.reshape(x.shape[0], nc, nxh, nz, x.shape[-1])
    y = jnp.take(jnp.take(y, c_idx, axis=1), xh_idx, axis=2)
    return jnp.transpose(y, (0, 3, 2, 1, 4)).reshape(x.shape)


def reduce_scatter_head(x, head_sizes):
    ny, nxl = head_sizes
    rows, width = x.shape
    xl = lax.axis_index("xl")
    y = lax.axis_index("y")
    grouped = x.reshape(rows, ny, nxl, width // (ny * nxl))
    kept = jnp.take(grouped, xl, axis=2)
    sent = jnp.take(grouped, (xl + 1) % nxl, axis=2).astype(jnp.bfloat16)
    summed = kept + lax.ppermute(sent, "xl", [(0, 1), (1, 0)]).astype(jnp.float32)
    acc = jnp.take(summed, y, axis=1)
    for shift in range(1, ny):
        piece = jnp.take(summed, (y + shift) % ny, axis=1).astype(jnp.bfloat16)
        acc = acc + lax.ppermute(
            piece, "y", [(i, (i + shift) % ny) for i in range(ny)]
        ).astype(jnp.float32)
    return acc


def make_local(sizes, head_sizes):
    nz, nxh, nc = sizes
    nctx = nz * nxh * nc

    def local(tokens, norm_gain, w_query, w_key, w_value, w_out, row_map, doc_lengths, doc_labels):
        tok_rows, width = tokens.shape
        d_rows = w_query.shape[0]
        q_cols = w_query.shape[1]
        kv_cols = w_key.shape[1]
        group_size = q_cols // kv_cols
        runs_here = tok_rows // RUN
        total_runs = runs_here * nctx
        win_runs = MOST // RUN + 1

        normed = rms_norm(tokens, norm_gain)
        doc_index, in_doc, doc_ends = doc_layout(row_map, doc_lengths)

        qkv_cols = q_cols + 2 * kv_cols
        out_cols = w_out.shape[0]
        w_z = gather_z(jnp.concatenate([w_query, w_key, w_value, w_out.T], axis=1))
        w_o = gather_pair(w_z[:, qkv_cols:]).reshape(nctx, d_rows, out_cols)
        w_proj = w_z[:, :qkv_cols]

        pair = ("xh", "c")
        npair = nxh * nc
        me = lax.axis_index("xh") * nc + lax.axis_index("c")
        quarters = jnp.transpose(
            normed.reshape(tok_rows, nz, nxh, nc, d_rows), (0, 2, 3, 1, 4)
        ).reshape(tok_rows, npair, nz * d_rows)
        perms = [[(i, i ^ flip) for i in range(npair)] for flip in range(1, npair)]
        theirs = [
            lax.ppermute(jnp.take(quarters, me ^ flip, axis=1), pair, perm)
            for flip, perm in zip(range(1, npair), perms)
        ]
        stacked = jnp.concatenate([jnp.take(quarters, me, axis=1)] + theirs, axis=0)
        parts = jnp.dot(stacked, w_proj, preferred_element_type=jnp.float32)
        rows = tok_rows
        on_chip = lax.ppermute(
            jnp.concatenate([parts[rows : 2 * rows], parts[3 * rows : 4 * rows]]), pair, perms[0]
        )
        across = lax.ppermute(parts[2 * rows : 3 * rows] + on_chip[rows:], pair, perms[1])
        proj = parts[:rows] + on_chip[:rows] + across
        queries = proj[:, :q_cols].reshape(tok_rows, group_size, HEAD_DIM)
        key_proj = proj[:, q_cols : q_cols + kv_cols]
        value_proj = proj[:, q_cols + kv_cols :].astype(jnp.bfloat16)
        queries = rotate(queries, in_doc).astype(jnp.bfloat16)
        key_proj = rotate(key_proj, in_doc).astype(jnp.bfloat16)

        assert 2 * tok_rows == 2 * kv_cols
        pos_row = jnp.concatenate([row_map // RUN, row_map % RUN]).astype(jnp.bfloat16)[None, :]
        kv_buf = jnp.concatenate(
            [jnp.concatenate([key_proj, value_proj], axis=1), jnp.pad(pos_row, ((0, 7), (0, 0)))],
            axis=0,
        )
        kv = gather_pair(gather_z(kv_buf)).reshape(nctx, tok_rows + 8, 2 * kv_cols)
        pos_code = kv[:, tok_rows, :].astype(jnp.int32)
        key_pos_all = pos_code[:, :tok_rows] * RUN + pos_code[:, tok_rows:]
        kv_halves = kv[:, :tok_rows].reshape(total_runs, RUN, 2 * kv_cols)
        pos_halves = key_pos_all.reshape(total_runs, RUN)
        run_of_half = pos_halves[:, 0] // RUN
        half_of_run = jnp.zeros((total_runs,), jnp.int32).at[run_of_half].set(
            jnp.arange(total_runs, dtype=jnp.int32)
        )

        q_pos = row_map.reshape(runs_here, RUN)
        q_start = (row_map - in_doc).reshape(runs_here, RUN)
        q_run = q_pos[:, 0] // RUN
        first_run = jnp.maximum(q_run - (win_runs - 1), 0)
        win = first_run[:, None] + jnp.arange(win_runs, dtype=jnp.int32)[None, :]
        win_halves = half_of_run[win]
        kv_win = kv_halves[win_halves].reshape(runs_here, win_runs * RUN, 2 * kv_cols)
        k_pos = pos_halves[win_halves].reshape(runs_here, win_runs * RUN)
        k_win = kv_win[..., :kv_cols]
        v_win = kv_win[..., kv_cols:]

        q_runs = queries.reshape(runs_here, RUN, group_size, HEAD_DIM)
        scale_factor = HEAD_DIM ** (-0.5)
        scores = (
            jnp.einsum("rqgd,rkd->rgqk", q_runs, k_win, preferred_element_type=jnp.float32)
            * scale_factor
        )
        allowed = (k_pos[:, None, :] >= q_start[:, :, None]) & (k_pos[:, None, :] <= q_pos[:, :, None])
        allowed = allowed[:, None]
        scores = jnp.where(allowed, scores, NEG_FILL)
        row_top = jnp.max(scores, -1, keepdims=True)
        weights = jnp.where(allowed, jnp.exp(scores - row_top), 0.0)
        row_sum = jnp.sum(weights, -1, keepdims=True)
        mixed = (
            jnp.einsum(
                "rgqk,rkd->rgqd", weights.astype(jnp.bfloat16), v_win,
                preferred_element_type=jnp.float32,
            )
            / row_sum
        ).astype(jnp.bfloat16)
        attended = jnp.transpose(mixed, (0, 2, 1, 3)).reshape(tok_rows, q_cols)

        partial_g = jnp.einsum(
            "tk,jdk->tjd", attended, w_o,
            preferred_element_type=jnp.float32,
        )
        partial_out = from_gathered_order(partial_g, sizes).reshape(tok_rows, width)
        head_share = reduce_scatter_head(partial_out, head_sizes)
        col_width = head_share.shape[1]
        head_idx = lax.axis_index("y") * head_sizes[1] + lax.axis_index("xl")
        own_cols = lax.dynamic_slice_in_dim(tokens, head_idx * col_width, col_width, 1)
        residual_out = (own_cols.astype(jnp.float32) + head_share).astype(jnp.bfloat16)

        is_last = row_map[:, None] == (doc_ends - 1)[None, :]
        label_f = doc_labels.astype(jnp.float32)
        harmful = jnp.sum(label_f)
        harmless = doc_labels.shape[0] - jnp.sum(label_f)
        stream = residual_out.astype(jnp.float32)
        harm_rows = jnp.sum(jnp.where(is_last, label_f[None, :], 0.0), 1)
        safe_rows = jnp.sum(jnp.where(is_last, (1.0 - label_f)[None, :], 0.0), 1)
        sums = jnp.stack(
            [jnp.sum(harm_rows[:, None] * stream, 0), jnp.sum(safe_rows[:, None] * stream, 0)]
        )
        for axis in (("xh", "c"), "z"):
            sums = lax.psum(sums, axis)
        refusal_direction = sums[0] / harmful - sums[1] / harmless
        return (residual_out, refusal_direction)

    return local


def solution(mesh):
    n_ctx = mesh.shape["ctx"]
    n_head = mesh.shape["head"]
    nc, nxh = 2, 2
    nz = n_ctx // (nc * nxh)
    ny, nxl = n_head // 2, 2
    fine = Mesh(mesh.devices.reshape(nz, nxh, nc, ny, nxl), ("z", "xh", "c", "y", "xl"))
    placed = (
        P(CTX, None),
        P(),
        P(CTX, HEAD),
        P(CTX, HEAD),
        P(CTX, HEAD),
        P(HEAD, CTX),
        P(CTX),
        P(),
        P(),
    )
    return jax.shard_map(
        make_local((nz, nxh, nc), (ny, nxl)),
        mesh=fine,
        in_specs=placed,
        out_specs=(P(CTX, HEAD), P(HEAD)),
        check_vma=False,
    )
```

```python
import math

import jax
import jax.numpy as jnp
from jax import lax
from jax.sharding import Mesh
from jax.sharding import PartitionSpec as P

HEADS = 32
KV_HEADS = 8
HEAD_DIM = 128
MOST = 2048
RUN = 64

ROPE_BASE = 500000.0
NEG_FILL = -1e30

CTX = ("z", "xh", "c")
HEAD = ("y", "xl")


def doc_layout(row_map, doc_lengths):
    doc_ends = jnp.cumsum(doc_lengths)
    doc_starts = doc_ends - doc_lengths
    doc_index = jnp.sum((row_map[:, None] >= doc_ends[None, :]).astype(jnp.int32), 1)
    member = doc_index[:, None] == jnp.arange(doc_ends.shape[0], dtype=jnp.int32)[None, :]
    in_doc = row_map - jnp.sum(jnp.where(member, doc_starts[None, :], 0), 1)
    return (doc_index, in_doc, doc_ends)


def rotate(values, in_doc):
    head_dim = values.shape[-1]
    half_dim = head_dim // 2
    inv_freq = jnp.exp(
        jnp.arange(half_dim).astype(jnp.float32) * (-2.0 * math.log(ROPE_BASE) / head_dim)
    )
    angles = in_doc.astype(jnp.float32)[:, None] * inv_freq[None, :]
    shape_out = (angles.shape[0],) + (1,) * (values.ndim - 2) + (half_dim,)
    cosine = jnp.cos(angles).reshape(shape_out)
    sine_val = jnp.sin(angles).reshape(shape_out)
    front_half = values[..., :half_dim]
    back_half = values[..., half_dim:]
    return jnp.concatenate(
        [front_half * cosine - back_half * sine_val, back_half * cosine + front_half * sine_val], -1
    )


def rms_norm(tokens, norm_gain):
    wide_tokens = tokens.astype(jnp.float32)
    row_scale = lax.rsqrt(jnp.mean(wide_tokens * wide_tokens, -1, keepdims=True) + 1e-05)
    return (wide_tokens * row_scale * norm_gain).astype(jnp.bfloat16)


def swap_cat(x, axis_name):
    return jnp.concatenate([x, lax.ppermute(x, axis_name, [(0, 1), (1, 0)])], 0)


def gather_z(x):
    return lax.all_gather(x, "z", axis=0, tiled=True)


def gather_pair(x):
    return swap_cat(swap_cat(x, "xh"), "c")


def relative_index():
    return (
        lax.axis_index("c") ^ jnp.arange(2, dtype=jnp.int32),
        lax.axis_index("xh") ^ jnp.arange(2, dtype=jnp.int32),
    )


def to_gathered_order(x, sizes):
    nz, nxh, nc = sizes
    c_idx, xh_idx = relative_index()
    y = jnp.transpose(x.reshape(x.shape[0], nz, nxh, nc, x.shape[-1]), (0, 3, 2, 1, 4))
    y = jnp.take(jnp.take(y, c_idx, axis=1), xh_idx, axis=2)
    return y.reshape(x.shape)


def from_gathered_order(x, sizes):
    nz, nxh, nc = sizes
    c_idx, xh_idx = relative_index()
    y = x.reshape(x.shape[0], nc, nxh, nz, x.shape[-1])
    y = jnp.take(jnp.take(y, c_idx, axis=1), xh_idx, axis=2)
    return jnp.transpose(y, (0, 3, 2, 1, 4)).reshape(x.shape)


def reduce_scatter_head(x, head_sizes):
    ny, nxl = head_sizes
    rows, width = x.shape
    xl = lax.axis_index("xl")
    y = lax.axis_index("y")
    grouped = x.reshape(rows, ny, nxl, width // (ny * nxl))
    kept = jnp.take(grouped, xl, axis=2)
    sent = jnp.take(grouped, (xl + 1) % nxl, axis=2).astype(jnp.bfloat16)
    summed = kept + lax.ppermute(sent, "xl", [(0, 1), (1, 0)]).astype(jnp.float32)
    acc = jnp.take(summed, y, axis=1)
    for shift in range(1, ny):
        piece = jnp.take(summed, (y + shift) % ny, axis=1).astype(jnp.bfloat16)
        acc = acc + lax.ppermute(
            piece, "y", [(i, (i + shift) % ny) for i in range(ny)]
        ).astype(jnp.float32)
    return acc


def make_local(sizes, head_sizes):
    nz, nxh, nc = sizes
    nctx = nz * nxh * nc

    def local(tokens, norm_gain, w_query, w_key, w_value, w_out, row_map, doc_lengths, doc_labels):
        tok_rows, width = tokens.shape
        d_rows = w_query.shape[0]
        q_cols = w_query.shape[1]
        kv_cols = w_key.shape[1]
        group_size = q_cols // kv_cols
        runs_here = tok_rows // RUN
        total_runs = runs_here * nctx
        win_runs = MOST // RUN + 1

        normed = rms_norm(tokens, norm_gain)
        doc_index, in_doc, doc_ends = doc_layout(row_map, doc_lengths)

        qkv_cols = q_cols + 2 * kv_cols
        out_cols = w_out.shape[0]
        w_z = gather_z(jnp.concatenate([w_query, w_key, w_value, w_out.T], axis=1))
        w_o = gather_pair(w_z[:, qkv_cols:]).reshape(nctx, d_rows, out_cols)
        w_proj = w_z[:, :qkv_cols]

        pair = ("xh", "c")
        npair = nxh * nc
        me = lax.axis_index("xh") * nc + lax.axis_index("c")
        quarters = jnp.transpose(
            normed.reshape(tok_rows, nz, nxh, nc, d_rows), (0, 2, 3, 1, 4)
        ).reshape(tok_rows, npair, nz * d_rows)
        perms = [[(i, i ^ flip) for i in range(npair)] for flip in range(1, npair)]
        theirs = [
            lax.ppermute(jnp.take(quarters, me ^ flip, axis=1), pair, perm)
            for flip, perm in zip(range(1, npair), perms)
        ]
        stacked = jnp.concatenate([jnp.take(quarters, me, axis=1)] + theirs, axis=0)
        parts = jnp.dot(stacked, w_proj, preferred_element_type=jnp.float32)
        rows = tok_rows
        for_relay = lax.ppermute(parts[3 * rows : 4 * rows], pair, perms[0])
        across = lax.ppermute(parts[2 * rows : 3 * rows] + for_relay, pair, perms[1])
        on_chip = lax.ppermute(parts[rows : 2 * rows], pair, perms[0])
        proj = parts[:rows] + on_chip + across
        queries = proj[:, :q_cols].reshape(tok_rows, group_size, HEAD_DIM)
        key_proj = proj[:, q_cols : q_cols + kv_cols]
        value_proj = proj[:, q_cols + kv_cols :].astype(jnp.bfloat16)
        queries = rotate(queries, in_doc).astype(jnp.bfloat16)
        key_proj = rotate(key_proj, in_doc).astype(jnp.bfloat16)

        assert 2 * tok_rows == 2 * kv_cols
        pos_row = jnp.concatenate([row_map // RUN, row_map % RUN]).astype(jnp.bfloat16)[None, :]
        kv_buf = jnp.concatenate(
            [jnp.concatenate([key_proj, value_proj], axis=1), jnp.pad(pos_row, ((0, 7), (0, 0)))],
            axis=0,
        )
        kv = gather_pair(gather_z(kv_buf)).reshape(nctx, tok_rows + 8, 2 * kv_cols)
        pos_code = kv[:, tok_rows, :].astype(jnp.int32)
        key_pos_all = pos_code[:, :tok_rows] * RUN + pos_code[:, tok_rows:]
        kv_halves = kv[:, :tok_rows].reshape(total_runs, RUN, 2 * kv_cols)
        pos_halves = key_pos_all.reshape(total_runs, RUN)
        run_of_half = pos_halves[:, 0] // RUN
        half_of_run = jnp.zeros((total_runs,), jnp.int32).at[run_of_half].set(
            jnp.arange(total_runs, dtype=jnp.int32)
        )

        q_pos = row_map.reshape(runs_here, RUN)
        q_start = (row_map - in_doc).reshape(runs_here, RUN)
        q_run = q_pos[:, 0] // RUN
        first_run = jnp.maximum(q_run - (win_runs - 1), 0)
        win = first_run[:, None] + jnp.arange(win_runs, dtype=jnp.int32)[None, :]
        win_halves = half_of_run[win]
        kv_win = kv_halves[win_halves].reshape(runs_here, win_runs * RUN, 2 * kv_cols)
        k_pos = pos_halves[win_halves].reshape(runs_here, win_runs * RUN)
        k_win = kv_win[..., :kv_cols]
        v_win = kv_win[..., kv_cols:]

        q_runs = queries.reshape(runs_here, RUN, group_size, HEAD_DIM)
        scale_factor = HEAD_DIM ** (-0.5)
        scores = (
            jnp.einsum("rqgd,rkd->rgqk", q_runs, k_win, preferred_element_type=jnp.float32)
            * scale_factor
        )
        allowed = (k_pos[:, None, :] >= q_start[:, :, None]) & (k_pos[:, None, :] <= q_pos[:, :, None])
        allowed = allowed[:, None]
        scores = jnp.where(allowed, scores, NEG_FILL)
        row_top = jnp.max(scores, -1, keepdims=True)
        weights = jnp.where(allowed, jnp.exp(scores - row_top), 0.0)
        row_sum = jnp.sum(weights, -1, keepdims=True)
        mixed = (
            jnp.einsum(
                "rgqk,rkd->rgqd", weights.astype(jnp.bfloat16), v_win,
                preferred_element_type=jnp.float32,
            )
            / row_sum
        ).astype(jnp.bfloat16)
        attended = jnp.transpose(mixed, (0, 2, 1, 3)).reshape(tok_rows, q_cols)

        partial_g = jnp.einsum(
            "tk,jdk->tjd", attended, w_o,
            preferred_element_type=jnp.float32,
        )
        partial_out = from_gathered_order(partial_g, sizes).reshape(tok_rows, width)
        head_share = reduce_scatter_head(partial_out, head_sizes)
        col_width = head_share.shape[1]
        head_idx = lax.axis_index("y") * head_sizes[1] + lax.axis_index("xl")
        own_cols = lax.dynamic_slice_in_dim(tokens, head_idx * col_width, col_width, 1)
        residual_out = (own_cols.astype(jnp.float32) + head_share).astype(jnp.bfloat16)

        is_last = row_map[:, None] == (doc_ends - 1)[None, :]
        label_f = doc_labels.astype(jnp.float32)
        harmful = jnp.sum(label_f)
        harmless = doc_labels.shape[0] - jnp.sum(label_f)
        stream = residual_out.astype(jnp.float32)
        harm_rows = jnp.sum(jnp.where(is_last, label_f[None, :], 0.0), 1)
        safe_rows = jnp.sum(jnp.where(is_last, (1.0 - label_f)[None, :], 0.0), 1)
        sums = jnp.stack(
            [jnp.sum(harm_rows[:, None] * stream, 0), jnp.sum(safe_rows[:, None] * stream, 0)]
        )
        for axis in ("c", "xh", "z"):
            sums = lax.psum(sums, axis)
        refusal_direction = sums[0] / harmful - sums[1] / harmless
        return (residual_out, refusal_direction)

    return local


def solution(mesh):
    n_ctx = mesh.shape["ctx"]
    n_head = mesh.shape["head"]
    nc, nxh = 2, 2
    nz = n_ctx // (nc * nxh)
    ny, nxl = n_head // 2, 2
    fine = Mesh(mesh.devices.reshape(nz, nxh, nc, ny, nxl), ("z", "xh", "c", "y", "xl"))
    placed = (
        P(CTX, None),
        P(),
        P(CTX, HEAD),
        P(CTX, HEAD),
        P(CTX, HEAD),
        P(HEAD, CTX),
        P(CTX),
        P(),
        P(),
    )
    return jax.shard_map(
        make_local((nz, nxh, nc), (ny, nxl)),
        mesh=fine,
        in_specs=placed,
        out_specs=(P(CTX, HEAD), P(HEAD)),
        check_vma=False,
    )
```
